32 devices in a mesh: grp: 8 (over y, x, core), ent: 4 (over z).
Axes of the slice: x: 2, y: 2, z: 4, core: 2. Of those that a mesh axis runs over, the one named last changes fastest.
Arguments:
- factor: bfloat16 [4096, 256], P(('grp', 'ent')), may hold values from -1.5 to 1.5
- cores: bfloat16 [16, 256, 256], replicated, may hold values from -0.375 to 0.375
- adjacency: int32 [768, 128, 128], P(('grp', 'ent')), may hold values 0 or 1
- tile_rels: int32 [32, 24], P(('grp', 'ent')), may hold values from 0 to 15
- tile_count: int32 [32], P(('grp', 'ent')), may hold values from 1 to 24, 480 in all
- send_lists: int32 [32, 4, 6], P(('grp', 'ent')), may hold values from 0 to 7
Outputs:
- factor_grad: float32 [4096, 256], P(('grp', 'ent'))
The draws below stay inside these ranges and needn't reach their ends.
All inputs are finite; a program needn't handle non-finite values. No bound on the sum of `adjacency` or of `tile_count` on one device may be relied on, other than what follows from the above.
Results may differ from the reference program's by a relative error of at most 0.002.
Values may be sent and summed in bfloat16 or wider, within the bound.
No kernel may reach another device: no remote copies, remote signals or barrier semaphores. Data moves between devices by JAX's collectives and lax.ppermute only.
A program may use at most 64 MiB of HBM per device.

```python
import math
import jax
import jax.numpy as jnp
import numpy as np
from jax import lax

RANK = 256
NREL = 16
BLOCK = 128
TILES = 24
CAP = 6
ENTITIES = 4096
N_GRP = 8
N_ENT = 4
DEVICES = 32


def place_ends(drawn, stream_key, smallest, top_value):
    spot = [jax.random.randint(jax.random.fold_in(stream_key, axis), (), 0, length) for axis, length in enumerate(drawn.shape)]
    main_axis = drawn.shape.index(max(drawn.shape))
    beside = spot[:main_axis] + [(spot[main_axis] + 1) % drawn.shape[main_axis]] + spot[main_axis + 1:]
    return drawn.at[tuple(spot)].set(smallest).at[tuple(beside)].set(top_value)


def shard_levels(rng, shape, split, least, high):
    factor_of = 1.0
    for position, blocks in split:
        heights = jax.random.uniform(jax.random.fold_in(jax.random.fold_in(rng, 6), position), (blocks,), jnp.float32, least / len(split), high / len(split))
        factor_of = factor_of * jnp.repeat(jnp.exp(heights), shape[position] // blocks).reshape((-1,) + (1,) * (len(shape) - 1 - position))
    return factor_of


def split_up(number_of, total, most, slope):
    loads = [(1 << 20) // math.isqrt(grade ** slope) + 1 for grade in range(2, number_of + 1)]
    surplus, counts = total - most - (number_of - 1), [1] * (number_of - 1)
    while surplus > 0:
        movable = [i for i in range(number_of - 1) if counts[i] < most]
        whole, remaining = sum([loads[i] for i in movable]), surplus
        for i in movable:
            addition = min(most - counts[i], max(1, remaining * loads[i] // whole), surplus)
            counts[i] = counts[i] + addition
            surplus = surplus - addition
    return np.array([most] + counts)


def uneven(own_key, count, total, most, slope):
    if count == 2:
        one = jax.random.randint(own_key, (), max(1, total - most), min(most, total - 1) + 1)
        return jnp.stack([one, total - one])
    tallies = jnp.asarray(split_up(count, total, most, slope), jnp.int32)
    pairs = (count - 1) // 2
    donor, receiver = tallies[1:1 + 2 * pairs:2], tallies[2:2 + 2 * pairs:2]
    slack = jnp.minimum(donor - 1, most - receiver)
    shifted = jax.random.randint(jax.random.fold_in(own_key, 1), (pairs,), 0, 1 << 20) % (slack + 1)
    tallies = tallies.at[1:1 + 2 * pairs:2].set(donor - shifted).at[2:2 + 2 * pairs:2].set(receiver + shifted)
    return tallies[jax.random.permutation(jax.random.fold_in(own_key, 2), count)]


def centred(key, dims, deviation, limit, shards=(), kind=jnp.bfloat16):
    result = jax.random.normal(key, dims, jnp.float32) * deviation
    if len(shards) > 0:
        result = shard_levels(key, dims, shards, -0.22, 0.18) * result
    return jnp.clip(result, min=-limit, max=limit).astype(kind)


def setup_inputs(seed: int = 0) -> dict:
    seeds = jax.random.split(jax.random.key(seed), 7)
    factor = centred(seeds[0], (ENTITIES, RANK), 0.25, 1.5, ((0, 32),))
    cores = centred(seeds[1], (NREL, RANK, RANK), RANK ** -0.5, 0.375)
    adjacency = place_ends((jax.random.randint(seeds[2], (DEVICES * TILES, BLOCK, BLOCK), 0, 2) < 1).astype(jnp.int32), jax.random.fold_in(seeds[2], 1), 0, 1)
    tile_rels = place_ends(jax.random.randint(seeds[3], (DEVICES, TILES), 0, NREL), jax.random.fold_in(seeds[3], 1), 0, NREL - 1).astype(jnp.int32)
    tile_count = uneven(seeds[4], DEVICES, DEVICES * TILES * 5 // 8, TILES, 2).astype(jnp.int32)
    send_lists = place_ends(jax.random.randint(seeds[5], (DEVICES, N_ENT, CAP), 0, N_GRP), jax.random.fold_in(seeds[5], 1), 0, N_GRP - 1).astype(jnp.int32)
    return dict(factor=factor, cores=cores, adjacency=adjacency, tile_rels=tile_rels, tile_count=tile_count, send_lists=send_lists)


LOSS_SCALE = 0.0625


def reference(factor, cores, adjacency, tile_rels, tile_count, send_lists):
    blocks = factor.reshape(DEVICES, BLOCK, RANK)
    device_ids = jnp.arange(DEVICES, dtype=jnp.int32)[:, None]
    tile_ids = jnp.arange(TILES, dtype=jnp.int32)[None, :]
    group_of = device_ids // N_ENT
    ent_of = device_ids % N_ENT
    relay = (ent_of + tile_ids) % N_ENT
    source = send_lists[(group_of * N_ENT + relay).astype(jnp.int32), jnp.broadcast_to(ent_of, relay.shape), jnp.broadcast_to(tile_ids // N_ENT, relay.shape)]
    columns = (source * N_ENT + relay).astype(jnp.int32)
    live = (tile_ids < tile_count[:, None]).astype(jnp.float32)
    adjacent_all = adjacency.reshape(DEVICES, TILES, BLOCK, BLOCK)
    highest_precision = lax.Precision.HIGHEST
    cores_wide = cores.astype(jnp.float32)

    def one_device(col_acc, inputs):
        own, cols, rels, alive, adjacent = inputs
        mapped_all = jnp.einsum('br,krs->kbs', own.astype(jnp.float32), cores_wide, precision=highest_precision).astype(jnp.bfloat16)
        mapped_tiles = mapped_all[rels].astype(jnp.float32)
        factor_panels = blocks[cols].astype(jnp.float32)
        predicted_scores = jnp.einsum('ogj,omj->ogm', mapped_tiles, factor_panels, precision=highest_precision)
        score_residual = ((predicted_scores - adjacent.astype(jnp.float32)) * (LOSS_SCALE * alive)[:, None, None]).astype(jnp.bfloat16).astype(jnp.float32)
        relation_product = jnp.einsum('xmw,xwe->xme', score_residual, factor_panels, precision=highest_precision).astype(jnp.bfloat16).astype(jnp.float32)
        row_part = jnp.einsum('tbs,trs->br', relation_product, cores_wide[rels], precision=highest_precision)
        gradient_terms = jnp.einsum('yzj,yzh->yjh', score_residual, mapped_tiles, precision=highest_precision).astype(jnp.bfloat16).astype(jnp.float32)
        col_acc = col_acc.at[cols].add(gradient_terms)
        return col_acc, row_part

    start = jnp.zeros((DEVICES, BLOCK, RANK), jnp.float32)
    col_acc, rows = lax.scan(one_device, start, (blocks, columns, tile_rels, live, adjacent_all))
    return (rows + col_acc).reshape(DEVICES * BLOCK, RANK)
```

```python
import jax
import jax.numpy as jnp
from jax import lax
from jax.sharding import PartitionSpec as P

LOSS_SCALE = 0.0625


def grp_reduce_scatter(parts, grp_count):
    if grp_count & (grp_count - 1):
        return lax.psum_scatter(parts, "grp", scatter_dimension=0, tiled=True)[0]
    me = lax.axis_index("grp")
    bit = 1
    while bit < grp_count:
        half = parts.reshape((parts.shape[0] // 2, 2) + parts.shape[1:])
        mine = (me // bit) % 2
        keep = jnp.where(mine == 0, half[:, 0], half[:, 1])
        send = jnp.where(mine == 0, half[:, 1], half[:, 0])
        got = lax.ppermute(send, "grp", [(i, i ^ bit) for i in range(grp_count)])
        parts = keep + got
        bit *= 2
    return parts[0]


def on_device(factor, cores, adjacency, tile_rels, tile_count, send_lists):
    ent_count = lax.axis_size("ent")
    grp_count = lax.axis_size("grp")
    my_ent = lax.axis_index("ent")
    tiles = tile_rels.shape[1]
    block = factor.shape[0]
    width = factor.shape[1]
    per_relay = tiles // ent_count
    lanes = block
    head_rows = 16

    tile_ids = jnp.arange(tiles, dtype=jnp.int32)
    live = (tile_ids < tile_count[0]).astype(jnp.float32)
    relay_ids = jnp.arange(ent_count, dtype=jnp.int32)
    slot_ids = jnp.arange(per_relay, dtype=jnp.int32)
    tile_of = slot_ids[None, :] * ent_count + (relay_ids[:, None] - my_ent) % ent_count
    adj_out = adjacency.astype(jnp.bfloat16)[tile_of].reshape(ent_count, per_relay * block, lanes)
    own_out = jnp.broadcast_to(
        factor.reshape(1, block * width // lanes, lanes), (ent_count, block * width // lanes, lanes)
    )
    head = jnp.concatenate(
        [tile_rels[0][tile_of].astype(jnp.float32), live[tile_of]], axis=1
    )
    head = jnp.pad(head, ((0, 0), (0, lanes - 2 * per_relay)))
    head = jnp.broadcast_to(head[:, None, :], (ent_count, head_rows, lanes)).astype(jnp.bfloat16)
    outgoing = jnp.concatenate([adj_out, own_out, head], axis=1)
    arrived = lax.all_to_all(outgoing, "ent", split_axis=0, concat_axis=0, tiled=True)

    adj_in = arrived[:, : per_relay * block].reshape(ent_count * per_relay, block, block)
    src_f = arrived[:, per_relay * block : per_relay * block + block * width // lanes].reshape(
        ent_count, block, width
    )
    head_in = arrived[:, -head_rows].astype(jnp.float32)
    rels = head_in[:, :per_relay].astype(jnp.int32).reshape(ent_count * per_relay)
    alive = head_in[:, per_relay : 2 * per_relay].reshape(ent_count * per_relay)
    groups = send_lists[0].reshape(ent_count * per_relay)

    group_blocks = lax.all_gather(factor, "grp", axis=0, tiled=False)
    panels = group_blocks[groups]
    core_tiles = cores[rels]
    src_tiles = jnp.repeat(src_f, per_relay, axis=0)
    mapped = jnp.einsum(
        "tbr,trs->tbs", src_tiles, core_tiles, preferred_element_type=jnp.float32
    ).astype(jnp.bfloat16)
    predicted = jnp.einsum("tgj,tmj->tgm", mapped, panels, preferred_element_type=jnp.float32)
    resid = (
        (predicted - adj_in.astype(jnp.float32)) * (LOSS_SCALE * alive)[:, None, None]
    ).astype(jnp.bfloat16)
    product = jnp.einsum(
        "tmw,twe->tme", resid, panels, preferred_element_type=jnp.float32
    ).astype(jnp.bfloat16)
    row_parts = jnp.einsum(
        "ejbs,ejrs->ebr",
        product.reshape(ent_count, per_relay, block, width),
        core_tiles.reshape(ent_count, per_relay, width, width),
        preferred_element_type=jnp.float32,
    )
    column_terms = jnp.einsum(
        "tzj,tzh->tjh", resid, mapped, preferred_element_type=jnp.float32
    ).astype(jnp.bfloat16)
    owner_onehot = (groups[:, None] == jnp.arange(grp_count, dtype=jnp.int32)[None, :]).astype(
        jnp.float32
    )
    owner_terms = jnp.dot(
        owner_onehot.T,
        column_terms.reshape(ent_count * per_relay, block * width).astype(jnp.float32),
        precision=lax.Precision.HIGHEST,
        preferred_element_type=jnp.float32,
    ).reshape(grp_count, block, width)

    rows_back = lax.all_to_all(row_parts, "ent", split_axis=0, concat_axis=0, tiled=True)
    owner_part = grp_reduce_scatter(owner_terms, grp_count)
    return rows_back.sum(axis=0) + owner_part


def solution(mesh):
    in_specs = (
        P(("grp", "ent"), None),
        P(),
        P(("grp", "ent"), None, None),
        P(("grp", "ent"), None),
        P(("grp", "ent")),
        P(("grp", "ent"), None, None),
    )
    out_specs = P(("grp", "ent"), None)
    return jax.shard_map(
        on_device, mesh=mesh, in_specs=in_specs, out_specs=out_specs, check_vma=False
    )
```

```python
import jax
import jax.numpy as jnp
from jax import lax
from jax.sharding import PartitionSpec as P

LOSS_SCALE = 0.0625


def grp_reduce_scatter(parts, grp_count):
    if grp_count & (grp_count - 1):
        return lax.psum_scatter(parts, "grp", scatter_dimension=0, tiled=True)[0]
    me = lax.axis_index("grp")
    bit = 1
    while bit < grp_count:
        half = parts.reshape((parts.shape[0] // 2, 2) + parts.shape[1:])
        mine = (me // bit) % 2
        keep = jnp.where(mine == 0, half[:, 0], half[:, 1])
        send = jnp.where(mine == 0, half[:, 1], half[:, 0])
        got = lax.ppermute(send, "grp", [(i, i ^ bit) for i in range(grp_count)])
        parts = keep + got
        bit *= 2
    return parts[0]


def grp_gather(block, grp_count):
    if grp_count & (grp_count - 1):
        return lax.all_gather(block, "grp", axis=0, tiled=False)
    me = lax.axis_index("grp")
    held = block[None]
    bit = 1
    while bit < grp_count:
        got = lax.ppermute(held, "grp", [(i, i ^ bit) for i in range(grp_count)])
        low = (me // bit) % 2 == 0
        held = jnp.where(
            low, jnp.concatenate([held, got], axis=0), jnp.concatenate([got, held], axis=0)
        )
        bit *= 2
    return held


def shift_ent(x, shift, ent_count):
    if shift % ent_count == 0:
        return x
    return lax.ppermute(x, "ent", [(i, (i + shift) % ent_count) for i in range(ent_count)])


def on_device(factor, cores, adjacency, tile_rels, tile_count, send_lists):
    ent_count = lax.axis_size("ent")
    grp_count = lax.axis_size("grp")
    my_ent = lax.axis_index("ent")
    tiles = tile_rels.shape[1]
    block = factor.shape[0]
    width = factor.shape[1]
    per_relay = tiles // ent_count
    head_rows = 16
    chunks = 2 if per_relay % 2 == 0 else 1
    per_chunk = per_relay // chunks

    tile_ids = jnp.arange(tiles, dtype=jnp.int32)
    live = (tile_ids < tile_count[0]).astype(jnp.float32).reshape(per_relay, ent_count)
    rels_by_shift = tile_rels[0].reshape(per_relay, ent_count)
    adj_by_shift = adjacency.reshape(per_relay, ent_count, block, block)
    sent_heads = []
    sent_adj = []
    for k in range(ent_count):
        head = jnp.concatenate(
            [rels_by_shift[:, k].astype(jnp.float32), live[:, k]], axis=0
        )
        head = jnp.pad(head, (0, width - 2 * per_relay))
        head = jnp.broadcast_to(head[None, :], (head_rows, width)).astype(jnp.bfloat16)
        sent_heads.append(shift_ent(jnp.concatenate([factor, head], axis=0), k, ent_count))
        sent_adj.append(
            [
                shift_ent(
                    adj_by_shift[c * per_chunk : (c + 1) * per_chunk, k].astype(jnp.bfloat16),
                    k,
                    ent_count,
                )
                for c in range(chunks)
            ]
        )

    group_blocks = grp_gather(factor, grp_count)
    routes = send_lists[0]
    src_of = (my_ent - jnp.arange(ent_count, dtype=jnp.int32)) % ent_count
    groups_all = routes[src_of]
    src_f = jnp.stack([h[:block] for h in sent_heads])
    heads = jnp.stack([h[block].astype(jnp.float32) for h in sent_heads])
    rels_all = heads[:, :per_relay].astype(jnp.int32)
    alive_all = heads[:, per_relay : 2 * per_relay]

    row_parts = jnp.zeros((ent_count, block, width), jnp.float32)
    owner_terms = jnp.zeros((grp_count, block, width), jnp.float32)
    for c in range(chunks):
        sl = slice(c * per_chunk, (c + 1) * per_chunk)
        count = ent_count * per_chunk
        adj_in = jnp.stack([a[c] for a in sent_adj]).reshape(count, block, block)
        rels = rels_all[:, sl].reshape(count)
        alive = alive_all[:, sl].reshape(count)
        groups = groups_all[:, sl].reshape(count)
        panels = group_blocks[groups]
        core_tiles = cores[rels]
        src_tiles = jnp.repeat(src_f, per_chunk, axis=0)
        mapped = jnp.einsum(
            "tbr,trs->tbs", src_tiles, core_tiles, preferred_element_type=jnp.float32
        ).astype(jnp.bfloat16)
        predicted = jnp.einsum(
            "tgj,tmj->tgm", mapped, panels, preferred_element_type=jnp.float32
        )
        resid = (
            (predicted - adj_in.astype(jnp.float32)) * (LOSS_SCALE * alive)[:, None, None]
        ).astype(jnp.bfloat16)
        product = jnp.einsum(
            "tmw,twe->tme", resid, panels, preferred_element_type=jnp.float32
        ).astype(jnp.bfloat16)
        row_parts = row_parts + jnp.einsum(
            "ejbs,ejrs->ebr",
            product.reshape(ent_count, per_chunk, block, width),
            core_tiles.reshape(ent_count, per_chunk, width, width),
            preferred_element_type=jnp.float32,
        )
        column_terms = jnp.einsum(
            "tzj,tzh->tjh", resid, mapped, preferred_element_type=jnp.float32
        ).astype(jnp.bfloat16)
        owner_onehot = (
            groups[:, None] == jnp.arange(grp_count, dtype=jnp.int32)[None, :]
        ).astype(jnp.float32)
        owner_terms = owner_terms + jnp.dot(
            owner_onehot.T,
            column_terms.reshape(count, block * width).astype(jnp.float32),
            precision=lax.Precision.HIGHEST,
            preferred_element_type=jnp.float32,
        ).reshape(grp_count, block, width)

    rows = row_parts[0]
    for k in range(1, ent_count):
        rows = rows + shift_ent(row_parts[k], -k, ent_count)
    owner_part = grp_reduce_scatter(owner_terms, grp_count)
    return rows + owner_part


def solution(mesh):
    in_specs = (
        P(("grp", "ent"), None),
        P(),
        P(("grp", "ent"), None, None),
        P(("grp", "ent"), None),
        P(("grp", "ent")),
        P(("grp", "ent"), None, None),
    )
    out_specs = P(("grp", "ent"), None)
    return jax.shard_map(
        on_device, mesh=mesh, in_specs=in_specs, out_specs=out_specs, check_vma=False
    )
```

```python
import jax
import jax.numpy as jnp
from jax import lax
from jax.experimental import pallas as pl
from jax.experimental.pallas import tpu as pltpu
from jax.sharding import PartitionSpec as P

LOSS_SCALE = 0.0625


def bit_reverse(values, bits):
    out = jnp.zeros_like(values)
    for b in range(bits):
        out = out | (((values >> b) & 1) << (bits - 1 - b))
    return out


def grp_reduce_scatter(parts, grp_count):
    me = lax.axis_index("grp")
    bit = 1
    while bit < grp_count:
        half = parts.reshape((2, parts.shape[0] // 2) + parts.shape[1:])
        mine = (me // bit) % 2
        keep = half[mine]
        send = half[1 - mine]
        got = lax.ppermute(send, "grp", [(i, i ^ bit) for i in range(grp_count)])
        parts = keep + got
        bit *= 2
    return parts[0]


def grp_gather(block, grp_count):
    me = lax.axis_index("grp")
    held = block[None]
    bit = 1
    while bit < grp_count:
        got = lax.ppermute(held, "grp", [(i, i ^ bit) for i in range(grp_count)])
        low = (me // bit) % 2 == 0
        held = jnp.where(
            low, jnp.concatenate([held, got], axis=0), jnp.concatenate([got, held], axis=0)
        )
        bit *= 2
    return held


def shift_ent(x, shift, ent_count):
    return lax.ppermute(x, "ent", [(i, (i + shift) % ent_count) for i in range(ent_count)])


def tile_kernel(rels_ref, groups_ref, slots_ref, alive_ref, adj_ref, src_ref, panel_ref, core_ref,
                row_ref, owner_ref, *, per_relay):
    t = pl.program_id(0)

    @pl.when(t == 0)
    def _():
        owner_ref[...] = jnp.zeros_like(owner_ref)

    @pl.when(t % per_relay == 0)
    def _():
        row_ref[...] = jnp.zeros_like(row_ref)

    own = src_ref[0]
    core = core_ref[0]
    panel = panel_ref[0]
    nt = (((1,), (1,)), ((), ()))
    mapped = jnp.dot(own, core, preferred_element_type=jnp.float32).astype(jnp.bfloat16)
    predicted = lax.dot_general(mapped, panel, nt, preferred_element_type=jnp.float32)
    scale = LOSS_SCALE * alive_ref[t].astype(jnp.float32)
    resid = ((predicted - adj_ref[0].astype(jnp.float32)) * scale).astype(jnp.bfloat16)
    product = jnp.dot(resid, panel, preferred_element_type=jnp.float32).astype(jnp.bfloat16)
    row_ref[0] += lax.dot_general(product, core, nt, preferred_element_type=jnp.float32)
    resid_t = resid.astype(jnp.float32).T.astype(jnp.bfloat16)
    column = jnp.dot(resid_t, mapped, preferred_element_type=jnp.float32).astype(jnp.bfloat16)
    slot = slots_ref[t]
    owner_ref[slot] += column.astype(jnp.float32)


def on_device(factor, cores, adjacency, tile_rels, tile_count, send_lists):
    ent_count = lax.axis_size("ent")
    grp_count = lax.axis_size("grp")
    my_ent = lax.axis_index("ent")
    tiles = tile_rels.shape[1]
    block = factor.shape[0]
    width = factor.shape[1]
    per_relay = tiles // ent_count
    head_rows = 16
    count = ent_count * per_relay
    grp_bits = grp_count.bit_length() - 1

    tile_ids = jnp.arange(tiles, dtype=jnp.int32)
    live = (tile_ids < tile_count.reshape(())).astype(jnp.float32)
    relay_ids = jnp.arange(ent_count, dtype=jnp.int32)
    slot_ids = jnp.arange(per_relay, dtype=jnp.int32)
    tile_of = slot_ids[None, :] * ent_count + (relay_ids[:, None] - my_ent) % ent_count
    adj_out = adjacency[tile_of].astype(jnp.bfloat16)
    head = jnp.concatenate(
        [tile_rels.reshape(tiles)[tile_of].astype(jnp.float32), live[tile_of]], axis=1
    )
    head = jnp.pad(head, ((0, 0), (0, width - 2 * per_relay)))
    head = jnp.broadcast_to(head[:, None, :], (ent_count, head_rows, width)).astype(jnp.bfloat16)
    own_out = jnp.concatenate(
        [jnp.broadcast_to(factor[None], (ent_count, block, width)), head], axis=1
    )
    adj_in = lax.all_to_all(adj_out, "ent", split_axis=0, concat_axis=0, tiled=True)
    own_in = lax.all_to_all(own_out, "ent", split_axis=0, concat_axis=0, tiled=True)
    group_blocks = grp_gather(factor, grp_count)

    heads = own_in[:, block].astype(jnp.float32)
    rels = heads[:, :per_relay].astype(jnp.int32).reshape(count)
    alive = heads[:, per_relay : 2 * per_relay].astype(jnp.int32).reshape(count)
    groups = send_lists.reshape(count)
    slots = bit_reverse(groups, grp_bits)

    grid_spec = pltpu.PrefetchScalarGridSpec(
        num_scalar_prefetch=4,
        grid=(count,),
        in_specs=[
            pl.BlockSpec((1, block, block), lambda t, r, g, s, a: (t, 0, 0)),
            pl.BlockSpec((1, block, width), lambda t, r, g, s, a: (t // per_relay, 0, 0)),
            pl.BlockSpec((1, block, width), lambda t, r, g, s, a: (g[t], 0, 0)),
            pl.BlockSpec((1, width, width), lambda t, r, g, s, a: (r[t], 0, 0)),
        ],
        out_specs=[
            pl.BlockSpec((1, block, width), lambda t, r, g, s, a: (t // per_relay, 0, 0)),
            pl.BlockSpec((grp_count, block, width), lambda t, r, g, s, a: (0, 0, 0)),
        ],
    )
    row_parts, owner_terms = pl.pallas_call(
        lambda *refs: tile_kernel(*refs, per_relay=per_relay),
        grid_spec=grid_spec,
        out_shape=[
            jax.ShapeDtypeStruct((ent_count, block, width), jnp.float32),
            jax.ShapeDtypeStruct((grp_count, block, width), jnp.float32),
        ],
    )(
        rels,
        groups,
        slots,
        alive,
        adj_in.reshape(count, block, block),
        own_in,
        group_blocks,
        cores,
    )

    rows = row_parts[my_ent]
    for k in range(1, ent_count):
        rows = rows + shift_ent(row_parts[(my_ent - k) % ent_count], -k, ent_count)
    owner_part = grp_reduce_scatter(owner_terms, grp_count)
    return (rows + owner_part)


def solution(mesh):
    in_specs = (
        P(("grp", "ent"), None),
        P(),
        P(("grp", "ent"), None, None),
        P(("grp", "ent"), None),
        P(("grp", "ent")),
        P(("grp", "ent"), None, None),
    )
    out_specs = P(("grp", "ent"), None)
    return jax.shard_map(
        on_device, mesh=mesh, in_specs=in_specs, out_specs=out_specs, check_vma=False
    )
```

```python
import jax
import jax.numpy as jnp
from jax import lax
from jax.experimental import pallas as pl
from jax.experimental.pallas import tpu as pltpu
from jax.sharding import PartitionSpec as P

LOSS_SCALE = 0.0625


def bit_reverse(values, bits):
    out = jnp.zeros_like(values)
    for b in range(bits):
        out = out | (((values >> b) & 1) << (bits - 1 - b))
    return out


def grp_reduce_scatter(parts, grp_count):
    me = lax.axis_index("grp")
    bit = 1
    while bit < grp_count:
        half = parts.reshape((2, parts.shape[0] // 2) + parts.shape[1:])
        mine = (me // bit) % 2
        keep = half[mine]
        send = half[1 - mine]
        got = lax.ppermute(send, "grp", [(i, i ^ bit) for i in range(grp_count)])
        parts = keep + got
        bit *= 2
    return parts[0]


def grp_gather(block, grp_count):
    me = lax.axis_index("grp")
    held = block[None]
    bit = 1
    while bit < grp_count:
        got = lax.ppermute(held, "grp", [(i, i ^ bit) for i in range(grp_count)])
        low = (me // bit) % 2 == 0
        held = jnp.where(
            low, jnp.concatenate([held, got], axis=0), jnp.concatenate([got, held], axis=0)
        )
        bit *= 2
    return held


def shift_ent(x, shift, ent_count):
    return lax.ppermute(x, "ent", [(i, (i + shift) % ent_count) for i in range(ent_count)])


def tile_kernel(rels_ref, groups_ref, slots_ref, alive_ref, in_ref, core_ref, panel_ref,
                row_ref, owner_ref, *, per_relay, block):
    e = pl.program_id(0)

    @pl.when(e == 0)
    def _():
        owner_ref[...] = jnp.zeros_like(owner_ref)

    nt = (((1,), (1,)), ((), ()))
    base = per_relay * block
    own_lo = in_ref[0, base : base + block, :]
    own_hi = in_ref[0, base + block : base + 2 * block, :]
    acc = None
    for j in range(per_relay):
        t = e * per_relay + j
        r = rels_ref[t]
        core = core_ref[r]
        panel = panel_ref[groups_ref[t]]
        mapped = (
            jnp.dot(own_lo, core[:block], preferred_element_type=jnp.float32)
            + jnp.dot(own_hi, core[block:], preferred_element_type=jnp.float32)
        ).astype(jnp.bfloat16)
        predicted = lax.dot_general(mapped, panel, nt, preferred_element_type=jnp.float32)
        scale = LOSS_SCALE * alive_ref[t].astype(jnp.float32)
        adj = in_ref[0, j * block : (j + 1) * block, :].astype(jnp.float32)
        resid = ((predicted - adj) * scale).astype(jnp.bfloat16)
        product = jnp.dot(resid, panel, preferred_element_type=jnp.float32).astype(jnp.bfloat16)
        part = lax.dot_general(product, core, nt, preferred_element_type=jnp.float32)
        acc = part if acc is None else acc + part
        resid_t = resid.astype(jnp.float32).T.astype(jnp.bfloat16)
        column = jnp.dot(resid_t, mapped, preferred_element_type=jnp.float32).astype(jnp.bfloat16)
        slot = slots_ref[t]
        owner_ref[slot] += column.astype(jnp.float32)
    row_ref[0] = acc


def on_device(factor, cores, adjacency, tile_rels, tile_count, send_lists):
    ent_count = lax.axis_size("ent")
    grp_count = lax.axis_size("grp")
    my_ent = lax.axis_index("ent")
    tiles = tile_rels.shape[1]
    block = factor.shape[0]
    width = factor.shape[1]
    per_relay = tiles // ent_count
    head_rows = 16
    count = ent_count * per_relay
    grp_bits = grp_count.bit_length() - 1
    relations = cores.shape[0]

    tile_ids = jnp.arange(tiles, dtype=jnp.int32)
    live = (tile_ids < tile_count.reshape(())).astype(jnp.float32)
    relay_ids = jnp.arange(ent_count, dtype=jnp.int32)
    slot_ids = jnp.arange(per_relay, dtype=jnp.int32)
    tile_of = slot_ids[None, :] * ent_count + (relay_ids[:, None] - my_ent) % ent_count
    adj_out = adjacency[tile_of].astype(jnp.bfloat16).reshape(ent_count, per_relay * block, block)
    halves = jnp.concatenate([factor[:, :block], factor[:, block:]], axis=0)
    head = jnp.concatenate(
        [tile_rels.reshape(tiles)[tile_of].astype(jnp.float32), live[tile_of]], axis=1
    )
    head = jnp.pad(head, ((0, 0), (0, block - 2 * per_relay)))
    head = jnp.broadcast_to(head[:, None, :], (ent_count, head_rows, block)).astype(jnp.bfloat16)
    outgoing = jnp.concatenate(
        [adj_out, jnp.broadcast_to(halves[None], (ent_count,) + halves.shape), head], axis=1
    )
    arrived = lax.all_to_all(outgoing, "ent", split_axis=0, concat_axis=0, tiled=True)
    group_blocks = grp_gather(factor, grp_count)

    heads = arrived[:, -head_rows].astype(jnp.float32)
    rels = heads[:, :per_relay].astype(jnp.int32).reshape(count)
    alive = heads[:, per_relay : 2 * per_relay].astype(jnp.int32).reshape(count)
    groups = send_lists.reshape(count)
    slots = bit_reverse(groups, grp_bits)
    rows_in = arrived.shape[1]

    grid_spec = pltpu.PrefetchScalarGridSpec(
        num_scalar_prefetch=4,
        grid=(ent_count,),
        in_specs=[
            pl.BlockSpec((1, rows_in, block), lambda e, r, g, s, a: (e, 0, 0)),
            pl.BlockSpec((relations, width, width), lambda e, r, g, s, a: (0, 0, 0)),
            pl.BlockSpec((grp_count, block, width), lambda e, r, g, s, a: (0, 0, 0)),
        ],
        out_specs=[
            pl.BlockSpec((1, block, width), lambda e, r, g, s, a: (e, 0, 0)),
            pl.BlockSpec((grp_count, block, width), lambda e, r, g, s, a: (0, 0, 0)),
        ],
    )
    row_parts, owner_terms = pl.pallas_call(
        lambda *refs: tile_kernel(*refs, per_relay=per_relay, block=block),
        grid_spec=grid_spec,
        out_shape=[
            jax.ShapeDtypeStruct((ent_count, block, width), jnp.float32),
            jax.ShapeDtypeStruct((grp_count, block, width), jnp.float32),
        ],
    )(rels, groups, slots, alive, arrived, cores, group_blocks)

    rows = row_parts[my_ent]
    for k in range(1, ent_count):
        rows = rows + shift_ent(row_parts[(my_ent - k) % ent_count], -k, ent_count)
    owner_part = grp_reduce_scatter(owner_terms, grp_count)
    return rows + owner_part


def solution(mesh):
    in_specs = (
        P(("grp", "ent"), None),
        P(),
        P(("grp", "ent"), None, None),
        P(("grp", "ent"), None),
        P(("grp", "ent")),
        P(("grp", "ent"), None, None),
    )
    out_specs = P(("grp", "ent"), None)
    return jax.shard_map(
        on_device, mesh=mesh, in_specs=in_specs, out_specs=out_specs, check_vma=False
    )
```

```python
import jax
import jax.numpy as jnp
from jax import lax
from jax.experimental import pallas as pl
from jax.experimental.pallas import tpu as pltpu
from jax.sharding import PartitionSpec as P

LOSS_SCALE = 0.0625


def bit_reverse(values, bits):
    out = jnp.zeros_like(values)
    for b in range(bits):
        out = out | (((values >> b) & 1) << (bits - 1 - b))
    return out


def grp_reduce_scatter(parts, grp_count):
    me = lax.axis_index("grp")
    bit = 1
    while bit < grp_count:
        half = parts.reshape((2, parts.shape[0] // 2) + parts.shape[1:])
        mine = (me // bit) % 2
        keep = half[mine]
        send = half[1 - mine]
        got = lax.ppermute(send, "grp", [(i, i ^ bit) for i in range(grp_count)])
        parts = keep + got
        bit *= 2
    return parts[0]


def grp_gather(block, grp_count):
    me = lax.axis_index("grp")
    held = block[None]
    bit = 1
    while bit < grp_count:
        got = lax.ppermute(held, "grp", [(i, i ^ bit) for i in range(grp_count)])
        low = (me // bit) % 2 == 0
        held = jnp.where(
            low, jnp.concatenate([held, got], axis=0), jnp.concatenate([got, held], axis=0)
        )
        bit *= 2
    return held


def shift_ent(x, shift, ent_count):
    return lax.ppermute(x, "ent", [(i, (i + shift) % ent_count) for i in range(ent_count)])


def tile_kernel(rels_ref, groups_ref, slots_ref, alive_ref, in_ref, core_ref, panel_ref,
                row_ref, owner_ref, *, per_relay, block):
    e = pl.program_id(0)

    @pl.when(e == 0)
    def _():
        owner_ref[...] = jnp.zeros_like(owner_ref)

    nt = (((1,), (1,)), ((), ()))
    base = per_relay * block
    own = jnp.concatenate(
        [in_ref[0, base : base + block, :], in_ref[0, base + block : base + 2 * block, :]], axis=1
    )
    ts = [e * per_relay + j for j in range(per_relay)]
    rels = [rels_ref[t] for t in ts]
    groups = [groups_ref[t] for t in ts]
    mapped = [
        jnp.dot(own, core_ref[r], preferred_element_type=jnp.float32).astype(jnp.bfloat16)
        for r in rels
    ]
    predicted = [
        lax.dot_general(m, panel_ref[g], nt, preferred_element_type=jnp.float32)
        for m, g in zip(mapped, groups)
    ]
    resids = []
    for j, t in enumerate(ts):
        scale = LOSS_SCALE * alive_ref[t].astype(jnp.float32)
        adj = in_ref[0, j * block : (j + 1) * block, :].astype(jnp.float32)
        resids.append(((predicted[j] - adj) * scale).astype(jnp.bfloat16))
    products = [
        jnp.dot(r, panel_ref[g], preferred_element_type=jnp.float32).astype(jnp.bfloat16)
        for r, g in zip(resids, groups)
    ]
    columns = [
        jnp.dot(
            r.astype(jnp.float32).T.astype(jnp.bfloat16), m, preferred_element_type=jnp.float32
        ).astype(jnp.bfloat16)
        for r, m in zip(resids, mapped)
    ]
    acc = None
    for p, r in zip(products, rels):
        part = lax.dot_general(p, core_ref[r], nt, preferred_element_type=jnp.float32)
        acc = part if acc is None else acc + part
    for c, t in zip(columns, ts):
        owner_ref[slots_ref[t]] += c.astype(jnp.float32)
    row_ref[0] = acc


def on_device(factor, cores, adjacency, tile_rels, tile_count, send_lists):
    ent_count = lax.axis_size("ent")
    grp_count = lax.axis_size("grp")
    my_ent = lax.axis_index("ent")
    tiles = tile_rels.shape[1]
    block = factor.shape[0]
    width = factor.shape[1]
    per_relay = tiles // ent_count
    head_rows = 16
    count = ent_count * per_relay
    grp_bits = grp_count.bit_length() - 1
    relations = cores.shape[0]

    tile_ids = jnp.arange(tiles, dtype=jnp.int32)
    live = (tile_ids < tile_count.reshape(())).astype(jnp.float32)
    relay_ids = jnp.arange(ent_count, dtype=jnp.int32)
    slot_ids = jnp.arange(per_relay, dtype=jnp.int32)
    tile_of = slot_ids[None, :] * ent_count + (relay_ids[:, None] - my_ent) % ent_count
    adj_out = adjacency[tile_of].astype(jnp.bfloat16).reshape(ent_count, per_relay * block, block)
    halves = jnp.concatenate([factor[:, :block], factor[:, block:]], axis=0)
    head = jnp.concatenate(
        [tile_rels.reshape(tiles)[tile_of].astype(jnp.float32), live[tile_of]], axis=1
    )
    head = jnp.pad(head, ((0, 0), (0, block - 2 * per_relay)))
    head = jnp.broadcast_to(head[:, None, :], (ent_count, head_rows, block)).astype(jnp.bfloat16)
    outgoing = jnp.concatenate(
        [adj_out, jnp.broadcast_to(halves[None], (ent_count,) + halves.shape), head], axis=1
    )
    arrived = lax.all_to_all(outgoing, "ent", split_axis=0, concat_axis=0, tiled=True)
    group_blocks = grp_gather(factor, grp_count)

    heads = arrived[:, -head_rows].astype(jnp.float32)
    rels = heads[:, :per_relay].astype(jnp.int32).reshape(count)
    alive = heads[:, per_relay : 2 * per_relay].astype(jnp.int32).reshape(count)
    groups = send_lists.reshape(count)
    slots = bit_reverse(groups, grp_bits)
    rows_in = arrived.shape[1]

    grid_spec = pltpu.PrefetchScalarGridSpec(
        num_scalar_prefetch=4,
        grid=(ent_count,),
        in_specs=[
            pl.BlockSpec((1, rows_in, block), lambda e, r, g, s, a: (e, 0, 0)),
            pl.BlockSpec((relations, width, width), lambda e, r, g, s, a: (0, 0, 0)),
            pl.BlockSpec((grp_count, block, width), lambda e, r, g, s, a: (0, 0, 0)),
        ],
        out_specs=[
            pl.BlockSpec((1, block, width), lambda e, r, g, s, a: (e, 0, 0)),
            pl.BlockSpec((grp_count, block, width), lambda e, r, g, s, a: (0, 0, 0)),
        ],
    )
    row_parts, owner_terms = pl.pallas_call(
        lambda *refs: tile_kernel(*refs, per_relay=per_relay, block=block),
        grid_spec=grid_spec,
        out_shape=[
            jax.ShapeDtypeStruct((ent_count, block, width), jnp.float32),
            jax.ShapeDtypeStruct((grp_count, block, width), jnp.float32),
        ],
    )(rels, groups, slots, alive, arrived, cores, group_blocks)

    rows = row_parts[my_ent]
    for k in range(1, ent_count):
        rows = rows + shift_ent(row_parts[(my_ent - k) % ent_count], -k, ent_count)
    owner_part = grp_reduce_scatter(owner_terms, grp_count)
    return rows + owner_part


def solution(mesh):
    in_specs = (
        P(("grp", "ent"), None),
        P(),
        P(("grp", "ent"), None, None),
        P(("grp", "ent"), None),
        P(("grp", "ent")),
        P(("grp", "ent"), None, None),
    )
    out_specs = P(("grp", "ent"), None)
    return jax.shard_map(
        on_device, mesh=mesh, in_specs=in_specs, out_specs=out_specs, check_vma=False
    )
```

```python
import jax
import jax.numpy as jnp
from jax import lax
from jax.experimental import pallas as pl
from jax.experimental.pallas import tpu as pltpu
from jax.sharding import PartitionSpec as P

LOSS_SCALE = 0.0625


def bit_reverse(values, bits):
    out = jnp.zeros_like(values)
    for b in range(bits):
        out = out | (((values >> b) & 1) << (bits - 1 - b))
    return out


def grp_reduce_scatter(parts, grp_count):
    bit = 1
    while bit < grp_count:
        half = parts.shape[0] // 2
        got = lax.ppermute(parts[half:], "grp", [(i, i ^ bit) for i in range(grp_count)])
        parts = parts[:half] + got
        bit *= 2
    return parts[0]


def grp_gather(block, grp_count):
    me = lax.axis_index("grp")
    held = block[None]
    bit = 1
    while bit < grp_count:
        got = lax.ppermute(held, "grp", [(i, i ^ bit) for i in range(grp_count)])
        low = (me // bit) % 2 == 0
        held = jnp.where(
            low, jnp.concatenate([held, got], axis=0), jnp.concatenate([got, held], axis=0)
        )
        bit *= 2
    return held


def shift_ent(x, shift, ent_count):
    return lax.ppermute(x, "ent", [(i, (i + shift) % ent_count) for i in range(ent_count)])


def tile_kernel(rels_ref, groups_ref, slots_ref, alive_ref, shift_ref, in_ref, core_ref, panel_ref,
                row_ref, owner_ref, *, per_relay, block):
    e = pl.program_id(0)

    @pl.when(e == 0)
    def _():
        owner_ref[...] = jnp.zeros_like(owner_ref)

    nt = (((1,), (1,)), ((), ()))
    base = per_relay * block
    own = jnp.concatenate(
        [in_ref[0, base : base + block, :], in_ref[0, base + block : base + 2 * block, :]], axis=1
    )
    ts = [e * per_relay + j for j in range(per_relay)]
    rels = [rels_ref[t] for t in ts]
    groups = [groups_ref[t] for t in ts]
    mapped = [
        jnp.dot(own, core_ref[r], preferred_element_type=jnp.float32).astype(jnp.bfloat16)
        for r in rels
    ]
    predicted = [
        lax.dot_general(m, panel_ref[g], nt, preferred_element_type=jnp.float32)
        for m, g in zip(mapped, groups)
    ]
    resids = []
    for j, t in enumerate(ts):
        scale = LOSS_SCALE * alive_ref[t].astype(jnp.float32)
        adj = in_ref[0, j * block : (j + 1) * block, :].astype(jnp.float32)
        resids.append(((predicted[j] - adj) * scale).astype(jnp.bfloat16))
    products = [
        jnp.dot(r, panel_ref[g], preferred_element_type=jnp.float32).astype(jnp.bfloat16)
        for r, g in zip(resids, groups)
    ]
    columns = [
        jnp.dot(
            r.astype(jnp.float32).T.astype(jnp.bfloat16), m, preferred_element_type=jnp.float32
        ).astype(jnp.bfloat16)
        for r, m in zip(resids, mapped)
    ]
    acc = None
    for p, r in zip(products, rels):
        part = lax.dot_general(p, core_ref[r], nt, preferred_element_type=jnp.float32)
        acc = part if acc is None else acc + part
    for c, t in zip(columns, ts):
        owner_ref[slots_ref[t]] += c.astype(jnp.float32)
    row_ref[0] = acc


def on_device(factor, cores, adjacency, tile_rels, tile_count, send_lists):
    ent_count = lax.axis_size("ent")
    grp_count = lax.axis_size("grp")
    my_ent = lax.axis_index("ent")
    tiles = tile_rels.shape[1]
    block = factor.shape[0]
    width = factor.shape[1]
    per_relay = tiles // ent_count
    head_rows = 16
    count = ent_count * per_relay
    grp_bits = grp_count.bit_length() - 1
    relations = cores.shape[0]

    tile_ids = jnp.arange(tiles, dtype=jnp.int32)
    live = (tile_ids < tile_count.reshape(())).astype(jnp.float32)
    relay_ids = jnp.arange(ent_count, dtype=jnp.int32)
    slot_ids = jnp.arange(per_relay, dtype=jnp.int32)
    tile_of = slot_ids[None, :] * ent_count + (relay_ids[:, None] - my_ent) % ent_count
    adj_out = adjacency[tile_of].astype(jnp.bfloat16).reshape(ent_count, per_relay * block, block)
    halves = jnp.concatenate([factor[:, :block], factor[:, block:]], axis=0)
    head = jnp.concatenate(
        [tile_rels.reshape(tiles)[tile_of].astype(jnp.float32), live[tile_of]], axis=1
    )
    head = jnp.pad(head, ((0, 0), (0, block - 2 * per_relay)))
    head = jnp.broadcast_to(head[:, None, :], (ent_count, head_rows, block)).astype(jnp.bfloat16)
    outgoing = jnp.concatenate(
        [adj_out, jnp.broadcast_to(halves[None], (ent_count,) + halves.shape), head], axis=1
    )
    arrived = lax.all_to_all(outgoing, "ent", split_axis=0, concat_axis=0, tiled=True)
    group_blocks = grp_gather(factor, grp_count)

    heads = arrived[:, -head_rows].astype(jnp.float32)
    rels = heads[:, :per_relay].astype(jnp.int32).reshape(count)
    alive = heads[:, per_relay : 2 * per_relay].astype(jnp.int32).reshape(count)
    groups = send_lists.reshape(count)
    slots = bit_reverse(groups ^ lax.axis_index("grp"), grp_bits)
    shifts = (my_ent - jnp.arange(ent_count, dtype=jnp.int32)) % ent_count
    rows_in = arrived.shape[1]

    grid_spec = pltpu.PrefetchScalarGridSpec(
        num_scalar_prefetch=5,
        grid=(ent_count,),
        in_specs=[
            pl.BlockSpec((1, rows_in, block), lambda e, r, g, s, a, k: (e, 0, 0)),
            pl.BlockSpec((relations, width, width), lambda e, r, g, s, a, k: (0, 0, 0)),
            pl.BlockSpec((grp_count, block, width), lambda e, r, g, s, a, k: (0, 0, 0)),
        ],
        out_specs=[
            pl.BlockSpec((1, block, width), lambda e, r, g, s, a, k: (k[e], 0, 0)),
            pl.BlockSpec((grp_count, block, width), lambda e, r, g, s, a, k: (0, 0, 0)),
        ],
    )
    row_parts, owner_terms = pl.pallas_call(
        lambda *refs: tile_kernel(*refs, per_relay=per_relay, block=block),
        grid_spec=grid_spec,
        out_shape=[
            jax.ShapeDtypeStruct((ent_count, block, width), jnp.float32),
            jax.ShapeDtypeStruct((grp_count, block, width), jnp.float32),
        ],
    )(rels, groups, slots, alive, shifts, arrived, cores, group_blocks)

    rows = row_parts[0]
    for k in range(1, ent_count):
        rows = rows + shift_ent(row_parts[k], -k, ent_count)
    owner_part = grp_reduce_scatter(owner_terms, grp_count)
    return rows + owner_part


def solution(mesh):
    in_specs = (
        P(("grp", "ent"), None),
        P(),
        P(("grp", "ent"), None, None),
        P(("grp", "ent"), None),
        P(("grp", "ent")),
        P(("grp", "ent"), None, None),
    )
    out_specs = P(("grp", "ent"), None)
    return jax.shard_map(
        on_device, mesh=mesh, in_specs=in_specs, out_specs=out_specs, check_vma=False
    )
```

```python
import jax
import jax.numpy as jnp
from jax import lax
from jax.experimental import pallas as pl
from jax.experimental.pallas import tpu as pltpu
from jax.sharding import PartitionSpec as P

LOSS_SCALE = 0.0625


def bit_reverse(values, bits):
    out = jnp.zeros_like(values)
    for b in range(bits):
        out = out | (((values >> b) & 1) << (bits - 1 - b))
    return out


def grp_reduce_scatter(parts, grp_count):
    bit = 1
    while bit < grp_count:
        half = parts.shape[0] // 2
        got = lax.ppermute(parts[half:], "grp", [(i, i ^ bit) for i in range(grp_count)])
        parts = parts[:half] + got
        bit *= 2
    return parts[0]


def grp_gather(block, grp_count):
    me = lax.axis_index("grp")
    held = block[None]
    bit = 1
    while bit < grp_count:
        got = lax.ppermute(held, "grp", [(i, i ^ bit) for i in range(grp_count)])
        low = (me // bit) % 2 == 0
        held = jnp.where(
            low, jnp.concatenate([held, got], axis=0), jnp.concatenate([got, held], axis=0)
        )
        bit *= 2
    return held


def shift_ent(x, shift, ent_count):
    return lax.ppermute(x, "ent", [(i, (i + shift) % ent_count) for i in range(ent_count)])


def tile_kernel(rels_ref, groups_ref, slots_ref, alive_ref, shift_ref, in_ref, core_ref, panel_ref,
                row_ref, owner_ref, *, per_relay, block):
    e = pl.program_id(0)

    @pl.when(e == 0)
    def _():
        owner_ref[...] = jnp.zeros_like(owner_ref)

    nt = (((1,), (1,)), ((), ()))
    base = per_relay * block
    own = jnp.concatenate(
        [in_ref[0, base : base + block, :], in_ref[0, base + block : base + 2 * block, :]], axis=1
    )
    ts = [e * per_relay + j for j in range(per_relay)]
    rels = [rels_ref[t] for t in ts]
    groups = [groups_ref[t] for t in ts]
    mapped = [
        jnp.dot(own, core_ref[r], preferred_element_type=jnp.float32).astype(jnp.bfloat16)
        for r in rels
    ]
    predicted = [
        lax.dot_general(m, panel_ref[g], nt, preferred_element_type=jnp.float32)
        for m, g in zip(mapped, groups)
    ]
    resids = []
    for j, t in enumerate(ts):
        scale = LOSS_SCALE * alive_ref[t].astype(jnp.float32)
        adj = in_ref[0, j * block : (j + 1) * block, :].astype(jnp.float32)
        resids.append(((predicted[j] - adj) * scale).astype(jnp.bfloat16))
    products = [
        jnp.dot(r, panel_ref[g], preferred_element_type=jnp.float32).astype(jnp.bfloat16)
        for r, g in zip(resids, groups)
    ]
    columns = [
        jnp.dot(
            r.astype(jnp.float32).T.astype(jnp.bfloat16), m, preferred_element_type=jnp.float32
        ).astype(jnp.bfloat16)
        for r, m in zip(resids, mapped)
    ]
    acc = None
    for p, r in zip(products, rels):
        part = lax.dot_general(p, core_ref[r], nt, preferred_element_type=jnp.float32)
        acc = part if acc is None else acc + part
    for c, t in zip(columns, ts):
        owner_ref[slots_ref[t]] += c.astype(jnp.float32)
    row_ref[0] = acc


def on_device(factor, cores, adjacency, tile_rels, tile_count, send_lists):
    ent_count = lax.axis_size("ent")
    grp_count = lax.axis_size("grp")
    my_ent = lax.axis_index("ent")
    tiles = tile_rels.shape[1]
    block = factor.shape[0]
    width = factor.shape[1]
    per_relay = tiles // ent_count
    head_rows = 16
    count = ent_count * per_relay
    grp_bits = grp_count.bit_length() - 1
    relations = cores.shape[0]

    relay_ids = jnp.arange(ent_count, dtype=jnp.int32)
    slot_ids = jnp.arange(per_relay, dtype=jnp.int32)
    tile_of = slot_ids[None, :] * ent_count + (relay_ids[:, None] - my_ent) % ent_count
    live = (tile_of < tile_count.reshape(())).astype(jnp.float32)
    start = (ent_count - my_ent) % ent_count

    def by_relay(x):
        doubled = jnp.concatenate([x, x], axis=1)
        return jnp.swapaxes(lax.dynamic_slice_in_dim(doubled, start, ent_count, axis=1), 0, 1)

    adj_out = by_relay(adjacency.reshape(per_relay, ent_count, block, block)).astype(
        jnp.bfloat16
    ).reshape(ent_count, per_relay * block, block)
    halves = jnp.concatenate([factor[:, :block], factor[:, block:]], axis=0)
    head = jnp.concatenate(
        [by_relay(tile_rels.reshape(per_relay, ent_count)).astype(jnp.float32), live], axis=1
    )
    head = jnp.pad(head, ((0, 0), (0, block - 2 * per_relay)))
    head = jnp.broadcast_to(head[:, None, :], (ent_count, head_rows, block)).astype(jnp.bfloat16)
    outgoing = jnp.concatenate(
        [adj_out, jnp.broadcast_to(halves[None], (ent_count,) + halves.shape), head], axis=1
    )
    arrived = lax.all_to_all(outgoing, "ent", split_axis=0, concat_axis=0, tiled=True)
    group_blocks = grp_gather(factor, grp_count)

    heads = arrived[:, -head_rows].astype(jnp.float32)
    rels = heads[:, :per_relay].astype(jnp.int32).reshape(count)
    alive = heads[:, per_relay : 2 * per_relay].astype(jnp.int32).reshape(count)
    groups = send_lists.reshape(count)
    slots = bit_reverse(groups ^ lax.axis_index("grp"), grp_bits)
    shifts = (my_ent - jnp.arange(ent_count, dtype=jnp.int32)) % ent_count
    rows_in = arrived.shape[1]

    grid_spec = pltpu.PrefetchScalarGridSpec(
        num_scalar_prefetch=5,
        grid=(ent_count,),
        in_specs=[
            pl.BlockSpec((1, rows_in, block), lambda e, r, g, s, a, k: (e, 0, 0)),
            pl.BlockSpec((relations, width, width), lambda e, r, g, s, a, k: (0, 0, 0)),
            pl.BlockSpec((grp_count, block, width), lambda e, r, g, s, a, k: (0, 0, 0)),
        ],
        out_specs=[
            pl.BlockSpec((1, block, width), lambda e, r, g, s, a, k: (k[e], 0, 0)),
            pl.BlockSpec((grp_count, block, width), lambda e, r, g, s, a, k: (0, 0, 0)),
        ],
    )
    row_parts, owner_terms = pl.pallas_call(
        lambda *refs: tile_kernel(*refs, per_relay=per_relay, block=block),
        grid_spec=grid_spec,
        out_shape=[
            jax.ShapeDtypeStruct((ent_count, block, width), jnp.float32),
            jax.ShapeDtypeStruct((grp_count, block, width), jnp.float32),
        ],
    )(rels, groups, slots, alive, shifts, arrived, cores, group_blocks)

    rows = row_parts[0]
    for k in range(1, ent_count):
        rows = rows + shift_ent(row_parts[k], -k, ent_count)
    owner_part = grp_reduce_scatter(owner_terms, grp_count)
    return rows + owner_part


def solution(mesh):
    in_specs = (
        P(("grp", "ent"), None),
        P(),
        P(("grp", "ent"), None, None),
        P(("grp", "ent"), None),
        P(("grp", "ent")),
        P(("grp", "ent"), None, None),
    )
    out_specs = P(("grp", "ent"), None)
    return jax.shard_map(
        on_device, mesh=mesh, in_specs=in_specs, out_specs=out_specs, check_vma=False
    )
```

```python
import jax
import jax.numpy as jnp
from jax import lax
from jax.experimental import pallas as pl
from jax.experimental.pallas import tpu as pltpu
from jax.sharding import PartitionSpec as P

LOSS_SCALE = 0.0625


def bit_reverse(values, bits):
    out = jnp.zeros_like(values)
    for b in range(bits):
        out = out | (((values >> b) & 1) << (bits - 1 - b))
    return out


def grp_reduce_scatter(parts, grp_count):
    bit = 1
    while bit < grp_count:
        half = parts.shape[0] // 2
        got = lax.ppermute(parts[half:], "grp", [(i, i ^ bit) for i in range(grp_count)])
        parts = parts[:half] + got
        bit *= 2
    return parts[0]


def grp_gather(block, grp_count):
    me = lax.axis_index("grp")
    held = block[None]
    bit = 1
    while bit < grp_count:
        got = lax.ppermute(held, "grp", [(i, i ^ bit) for i in range(grp_count)])
        low = (me // bit) % 2 == 0
        held = jnp.where(
            low, jnp.concatenate([held, got], axis=0), jnp.concatenate([got, held], axis=0)
        )
        bit *= 2
    return held


def shift_ent(x, shift, ent_count):
    return lax.ppermute(x, "ent", [(i, (i + shift) % ent_count) for i in range(ent_count)])


def tile_kernel(rels_ref, groups_ref, slots_ref, alive_ref, shift_ref, in_ref, core_ref, panel_ref,
                row_ref, owner_ref, *, per_relay, block):
    e = pl.program_id(0)

    @pl.when(e == 0)
    def _():
        owner_ref[...] = jnp.zeros_like(owner_ref)

    nt = (((1,), (1,)), ((), ()))
    base = per_relay * block
    own = jnp.concatenate(
        [in_ref[0, base : base + block, :], in_ref[0, base + block : base + 2 * block, :]], axis=1
    )
    ts = [e * per_relay + j for j in range(per_relay)]
    rels = [rels_ref[t] for t in ts]
    groups = [groups_ref[t] for t in ts]
    mapped = [
        jnp.dot(own, core_ref[r], preferred_element_type=jnp.float32).astype(jnp.bfloat16)
        for r in rels
    ]
    predicted = [
        lax.dot_general(m, panel_ref[g], nt, preferred_element_type=jnp.float32)
        for m, g in zip(mapped, groups)
    ]
    resids = []
    for j, t in enumerate(ts):
        scale = LOSS_SCALE * alive_ref[t].astype(jnp.float32)
        adj = in_ref[0, j * block : (j + 1) * block, :].astype(jnp.float32)
        resids.append(((predicted[j] - adj) * scale).astype(jnp.bfloat16))
    products = [
        jnp.dot(r, panel_ref[g], preferred_element_type=jnp.float32).astype(jnp.bfloat16)
        for r, g in zip(resids, groups)
    ]
    columns = [
        jnp.dot(
            r.astype(jnp.float32).T.astype(jnp.bfloat16), m, preferred_element_type=jnp.float32
        ).astype(jnp.bfloat16)
        for r, m in zip(resids, mapped)
    ]
    acc = None
    for p, r in zip(products, rels):
        part = lax.dot_general(p, core_ref[r], nt, preferred_element_type=jnp.float32)
        acc = part if acc is None else acc + part
    for c, t in zip(columns, ts):
        owner_ref[slots_ref[t]] += c.astype(jnp.float32)
    row_ref[0] = acc


def on_device(factor, cores, adjacency, tile_rels, tile_count, send_lists):
    ent_count = lax.axis_size("ent")
    grp_count = lax.axis_size("grp")
    my_ent = lax.axis_index("ent")
    tiles = tile_rels.shape[1]
    block = factor.shape[0]
    width = factor.shape[1]
    per_relay = tiles // ent_count
    head_rows = 16
    count = ent_count * per_relay
    grp_bits = grp_count.bit_length() - 1
    relations = cores.shape[0]

    tile_ids = jnp.arange(tiles, dtype=jnp.int32)
    live = (tile_ids < tile_count.reshape(())).astype(jnp.float32)
    relay_ids = jnp.arange(ent_count, dtype=jnp.int32)
    slot_ids = jnp.arange(per_relay, dtype=jnp.int32)
    tile_of = slot_ids[None, :] * ent_count + (relay_ids[:, None] - my_ent) % ent_count
    adj_out = adjacency[tile_of].astype(jnp.bfloat16).reshape(ent_count, per_relay * block, block)
    halves = jnp.concatenate([factor[:, :block], factor[:, block:]], axis=0)
    head = jnp.concatenate(
        [tile_rels.reshape(tiles)[tile_of].astype(jnp.float32), live[tile_of]], axis=1
    )
    head = jnp.pad(head, ((0, 0), (0, block - 2 * per_relay)))
    head = jnp.broadcast_to(head[:, None, :], (ent_count, head_rows, block)).astype(jnp.bfloat16)
    outgoing = jnp.concatenate(
        [adj_out, jnp.broadcast_to(halves[None], (ent_count,) + halves.shape), head], axis=1
    )
    arrived = lax.all_to_all(outgoing, "ent", split_axis=0, concat_axis=0, tiled=True)
    group_blocks = grp_gather(factor, grp_count)

    heads = arrived[:, -head_rows].astype(jnp.float32)
    rels = heads[:, :per_relay].astype(jnp.int32).reshape(count)
    alive = heads[:, per_relay : 2 * per_relay].astype(jnp.int32).reshape(count)
    groups = send_lists.reshape(count)
    slots = bit_reverse(groups ^ lax.axis_index("grp"), grp_bits)
    shifts = (my_ent - jnp.arange(ent_count, dtype=jnp.int32)) % ent_count
    rows_in = arrived.shape[1]

    grid_spec = pltpu.PrefetchScalarGridSpec(
        num_scalar_prefetch=5,
        grid=(ent_count,),
        in_specs=[
            pl.BlockSpec((1, rows_in, block), lambda e, r, g, s, a, k: (e, 0, 0)),
            pl.BlockSpec(memory_space=pltpu.VMEM),
            pl.BlockSpec(memory_space=pltpu.VMEM),
        ],
        out_specs=[
            pl.BlockSpec((1, block, width), lambda e, r, g, s, a, k: (k[e], 0, 0)),
            pl.BlockSpec((grp_count, block, width), lambda e, r, g, s, a, k: (0, 0, 0)),
        ],
    )
    row_parts, owner_terms = pl.pallas_call(
        lambda *refs: tile_kernel(*refs, per_relay=per_relay, block=block),
        grid_spec=grid_spec,
        out_shape=[
            jax.ShapeDtypeStruct((ent_count, block, width), jnp.float32),
            jax.ShapeDtypeStruct((grp_count, block, width), jnp.float32),
        ],
    )(rels, groups, slots, alive, shifts, arrived, cores, group_blocks)

    rows = row_parts[0]
    for k in range(1, ent_count):
        rows = rows + shift_ent(row_parts[k], -k, ent_count)
    owner_part = grp_reduce_scatter(owner_terms, grp_count)
    return rows + owner_part


def solution(mesh):
    in_specs = (
        P(("grp", "ent"), None),
        P(),
        P(("grp", "ent"), None, None),
        P(("grp", "ent"), None),
        P(("grp", "ent")),
        P(("grp", "ent"), None, None),
    )
    out_specs = P(("grp", "ent"), None)
    return jax.shard_map(
        on_device, mesh=mesh, in_specs=in_specs, out_specs=out_specs, check_vma=False
    )
```

```python
import jax
import jax.numpy as jnp
from jax import lax
from jax.experimental import pallas as pl
from jax.experimental.pallas import tpu as pltpu
from jax.sharding import PartitionSpec as P

LOSS_SCALE = 0.0625


def bit_reverse(values, bits):
    out = jnp.zeros_like(values)
    for b in range(bits):
        out = out | (((values >> b) & 1) << (bits - 1 - b))
    return out


def grp_reduce_scatter(keep, send, grp_count):
    parts = keep + lax.ppermute(send, "grp", [(i, i ^ 1) for i in range(grp_count)])
    bit = 2
    while bit < grp_count:
        half = parts.shape[0] // 2
        got = lax.ppermute(parts[half:], "grp", [(i, i ^ bit) for i in range(grp_count)])
        parts = parts[:half] + got
        bit *= 2
    return parts[0]


def grp_gather(block, grp_count):
    me = lax.axis_index("grp")
    held = block[None]
    bit = 1
    while bit < grp_count:
        got = lax.ppermute(held, "grp", [(i, i ^ bit) for i in range(grp_count)])
        low = (me // bit) % 2 == 0
        held = jnp.where(
            low, jnp.concatenate([held, got], axis=0), jnp.concatenate([got, held], axis=0)
        )
        bit *= 2
    return held


def shift_ent(x, shift, ent_count):
    return lax.ppermute(x, "ent", [(i, (i + shift) % ent_count) for i in range(ent_count)])


def tile_kernel(codes_ref, groups_ref, slots_ref, shift_ref, in_ref, core_ref, panel_ref,
                row_ref, keep_ref, send_ref, *, per_relay, block):
    e = pl.program_id(0)

    @pl.when(e == 0)
    def _():
        keep_ref[...] = jnp.zeros_like(keep_ref)
        send_ref[...] = jnp.zeros_like(send_ref)

    nt = (((1,), (1,)), ((), ()))
    base = per_relay * block
    own = jnp.concatenate(
        [in_ref[0, base : base + block, :], in_ref[0, base + block : base + 2 * block, :]], axis=1
    )
    half = keep_ref.shape[0]
    codes = [codes_ref[e, j] for j in range(per_relay)]
    rels = [c // 2 for c in codes]
    groups = [groups_ref[e, j] for j in range(per_relay)]
    mapped = [
        jnp.dot(own, core_ref[r], preferred_element_type=jnp.float32).astype(jnp.bfloat16)
        for r in rels
    ]
    predicted = [
        lax.dot_general(m, panel_ref[g], nt, preferred_element_type=jnp.float32)
        for m, g in zip(mapped, groups)
    ]
    resids = []
    for j in range(per_relay):
        scale = LOSS_SCALE * (codes[j] % 2).astype(jnp.float32)
        adj = in_ref[0, j * block : (j + 1) * block, :].astype(jnp.float32)
        resids.append(((predicted[j] - adj) * scale).astype(jnp.bfloat16))
    products = [
        jnp.dot(r, panel_ref[g], preferred_element_type=jnp.float32).astype(jnp.bfloat16)
        for r, g in zip(resids, groups)
    ]
    columns = [
        jnp.dot(
            r.astype(jnp.float32).T.astype(jnp.bfloat16), m, preferred_element_type=jnp.float32
        ).astype(jnp.bfloat16)
        for r, m in zip(resids, mapped)
    ]
    acc = None
    for p, r in zip(products, rels):
        part = lax.dot_general(p, core_ref[r], nt, preferred_element_type=jnp.float32)
        acc = part if acc is None else acc + part
    for j, c in enumerate(columns):
        slot = slots_ref[e, j]
        column = c.astype(jnp.float32)

        @pl.when(slot < half)
        def _():
            keep_ref[jnp.minimum(slot, half - 1)] += column

        @pl.when(slot >= half)
        def _():
            send_ref[jnp.maximum(slot - half, 0)] += column

    row_ref[0] = acc


def on_device(factor, cores, adjacency, tile_rels, tile_count, send_lists):
    ent_count = lax.axis_size("ent")
    grp_count = lax.axis_size("grp")
    my_ent = lax.axis_index("ent")
    tiles = tile_rels.shape[1]
    block = factor.shape[0]
    width = factor.shape[1]
    per_relay = tiles // ent_count
    head_rows = 16
    count = ent_count * per_relay
    grp_bits = grp_count.bit_length() - 1
    relations = cores.shape[0]

    tile_ids = jnp.arange(tiles, dtype=jnp.int32)
    live = (tile_ids < tile_count.reshape(())).astype(jnp.float32)
    relay_ids = jnp.arange(ent_count, dtype=jnp.int32)
    slot_ids = jnp.arange(per_relay, dtype=jnp.int32)
    tile_of = slot_ids[None, :] * ent_count + (relay_ids[:, None] - my_ent) % ent_count
    adj_out = adjacency[tile_of].astype(jnp.bfloat16).reshape(ent_count, per_relay * block, block)
    halves = jnp.concatenate([factor[:, :block], factor[:, block:]], axis=0)
    head = jnp.concatenate(
        [tile_rels.reshape(tiles)[tile_of].astype(jnp.float32), live[tile_of]], axis=1
    )
    head = jnp.pad(head, ((0, 0), (0, block - 2 * per_relay)))
    head = jnp.broadcast_to(head[:, None, :], (ent_count, head_rows, block)).astype(jnp.bfloat16)
    outgoing = jnp.concatenate(
        [adj_out, jnp.broadcast_to(halves[None], (ent_count,) + halves.shape), head], axis=1
    )
    arrived = lax.all_to_all(outgoing, "ent", split_axis=0, concat_axis=0, tiled=True)
    group_blocks = grp_gather(factor, grp_count)

    heads = arrived[:, -head_rows].astype(jnp.float32)
    codes = (heads[:, :per_relay] * 2 + heads[:, per_relay : 2 * per_relay]).astype(jnp.int32)
    groups = send_lists.reshape(ent_count, per_relay)
    slots = bit_reverse(groups ^ lax.axis_index("grp"), grp_bits)
    shifts = (my_ent - jnp.arange(ent_count, dtype=jnp.int32)) % ent_count
    rows_in = arrived.shape[1]

    grid_spec = pltpu.PrefetchScalarGridSpec(
        num_scalar_prefetch=4,
        grid=(ent_count,),
        in_specs=[
            pl.BlockSpec((1, rows_in, block), lambda e, c, g, s, k: (e, 0, 0)),
            pl.BlockSpec(memory_space=pltpu.VMEM),
            pl.BlockSpec(memory_space=pltpu.VMEM),
        ],
        out_specs=[
            pl.BlockSpec((1, block, width), lambda e, c, g, s, k: (k[e], 0, 0)),
            pl.BlockSpec((grp_count // 2, block, width), lambda e, c, g, s, k: (0, 0, 0)),
            pl.BlockSpec((grp_count // 2, block, width), lambda e, c, g, s, k: (0, 0, 0)),
        ],
    )
    row_parts, owner_keep, owner_send = pl.pallas_call(
        lambda *refs: tile_kernel(*refs, per_relay=per_relay, block=block),
        grid_spec=grid_spec,
        out_shape=[
            jax.ShapeDtypeStruct((ent_count, block, width), jnp.float32),
            jax.ShapeDtypeStruct((grp_count // 2, block, width), jnp.float32),
            jax.ShapeDtypeStruct((grp_count // 2, block, width), jnp.float32),
        ],
    )(codes, groups, slots, shifts, arrived, cores, group_blocks)

    rows = row_parts[0]
    for k in range(1, ent_count):
        rows = rows + shift_ent(row_parts[k], -k, ent_count)
    owner_part = grp_reduce_scatter(owner_keep, owner_send, grp_count)
    return rows + owner_part


def solution(mesh):
    in_specs = (
        P(("grp", "ent"), None),
        P(),
        P(("grp", "ent"), None, None),
        P(("grp", "ent"), None),
        P(("grp", "ent")),
        P(("grp", "ent"), None, None),
    )
    out_specs = P(("grp", "ent"), None)
    return jax.shard_map(
        on_device, mesh=mesh, in_specs=in_specs, out_specs=out_specs, check_vma=False
    )
```

```python
import jax
import jax.numpy as jnp
from jax import lax
from jax.experimental import pallas as pl
from jax.experimental.pallas import tpu as pltpu
from jax.sharding import PartitionSpec as P

LOSS_SCALE = 0.0625


def bit_reverse(values, bits):
    out = jnp.zeros_like(values)
    for b in range(bits):
        out = out | (((values >> b) & 1) << (bits - 1 - b))
    return out


def grp_reduce_scatter(keep, send, grp_count):
    parts = keep + lax.ppermute(send, "grp", [(i, i ^ 1) for i in range(grp_count)])
    bit = 2
    while bit < grp_count:
        half = parts.shape[0] // 2
        got = lax.ppermute(parts[half:], "grp", [(i, i ^ bit) for i in range(grp_count)])
        parts = parts[:half] + got
        bit *= 2
    return parts[0]


def grp_gather(block, grp_count):
    me = lax.axis_index("grp")
    held = block[None]
    bit = 1
    while bit < grp_count:
        got = lax.ppermute(held, "grp", [(i, i ^ bit) for i in range(grp_count)])
        low = (me // bit) % 2 == 0
        held = jnp.where(
            low, jnp.concatenate([held, got], axis=0), jnp.concatenate([got, held], axis=0)
        )
        bit *= 2
    return held


def shift_ent(x, shift, ent_count):
    return lax.ppermute(x, "ent", [(i, (i + shift) % ent_count) for i in range(ent_count)])


def tile_kernel(codes_ref, groups_ref, slots_ref, shift_ref, in_ref, core_ref, panel_ref,
                row_ref, keep_ref, send_ref, *, per_relay, block):
    e = pl.program_id(0)

    @pl.when(e == 0)
    def _():
        keep_ref[...] = jnp.zeros_like(keep_ref)
        send_ref[...] = jnp.zeros_like(send_ref)

    nt = (((1,), (1,)), ((), ()))
    base = per_relay * block
    own = jnp.concatenate(
        [in_ref[0, base : base + block, :], in_ref[0, base + block : base + 2 * block, :]], axis=1
    )
    half = keep_ref.shape[0]
    codes = [codes_ref[e, j] for j in range(per_relay)]
    rels = [c // 2 for c in codes]
    groups = [groups_ref[e, j] for j in range(per_relay)]
    mapped = [
        jnp.dot(own, core_ref[r], preferred_element_type=jnp.float32).astype(jnp.bfloat16)
        for r in rels
    ]
    predicted = [
        lax.dot_general(m, panel_ref[g], nt, preferred_element_type=jnp.float32)
        for m, g in zip(mapped, groups)
    ]
    resids = []
    for j in range(per_relay):
        scale = LOSS_SCALE * (codes[j] % 2).astype(jnp.float32)
        adj = in_ref[0, j * block : (j + 1) * block, :].astype(jnp.float32)
        resids.append(((predicted[j] - adj) * scale).astype(jnp.bfloat16))
    products = [
        jnp.dot(r, panel_ref[g], preferred_element_type=jnp.float32).astype(jnp.bfloat16)
        for r, g in zip(resids, groups)
    ]
    columns = [
        jnp.dot(
            r.astype(jnp.float32).T.astype(jnp.bfloat16), m, preferred_element_type=jnp.float32
        ).astype(jnp.bfloat16)
        for r, m in zip(resids, mapped)
    ]
    acc = None
    for p, r in zip(products, rels):
        part = lax.dot_general(p, core_ref[r], nt, preferred_element_type=jnp.float32)
        acc = part if acc is None else acc + part
    for j, c in enumerate(columns):
        slot = slots_ref[e, j]
        column = c.astype(jnp.float32)

        @pl.when(slot < half)
        def _():
            keep_ref[jnp.minimum(slot, half - 1)] += column

        @pl.when(slot >= half)
        def _():
            send_ref[jnp.maximum(slot - half, 0)] += column

    row_ref[0] = acc


def on_device(factor, cores, adjacency, tile_rels, tile_count, send_lists):
    ent_count = lax.axis_size("ent")
    grp_count = lax.axis_size("grp")
    my_ent = lax.axis_index("ent")
    tiles = tile_rels.shape[1]
    block = factor.shape[0]
    width = factor.shape[1]
    per_relay = tiles // ent_count
    head_rows = 16
    count = ent_count * per_relay
    grp_bits = grp_count.bit_length() - 1
    relations = cores.shape[0]

    relay_ids = jnp.arange(ent_count, dtype=jnp.int32)
    slot_ids = jnp.arange(per_relay, dtype=jnp.int32)
    tile_of = slot_ids[None, :] * ent_count + (relay_ids[:, None] - my_ent) % ent_count
    adj_out = adjacency[tile_of].astype(jnp.bfloat16).reshape(ent_count, per_relay * block, block)
    halves = jnp.concatenate([factor[:, :block], factor[:, block:]], axis=0)
    head = jnp.concatenate(
        [tile_rels.reshape(tiles)[tile_of].astype(jnp.float32),
         (tile_of < tile_count.reshape(())).astype(jnp.float32)],
        axis=1,
    )
    head = jnp.pad(head, ((0, 0), (0, block - 2 * per_relay)))
    head = jnp.broadcast_to(head[:, None, :], (ent_count, head_rows, block)).astype(jnp.bfloat16)
    outgoing = jnp.concatenate(
        [adj_out, jnp.broadcast_to(halves[None], (ent_count,) + halves.shape), head], axis=1
    )
    arrived = lax.all_to_all(outgoing, "ent", split_axis=0, concat_axis=0, tiled=True)
    group_blocks = grp_gather(factor, grp_count)

    heads = arrived[:, -head_rows].astype(jnp.float32)
    codes = (heads[:, :per_relay] * 2 + heads[:, per_relay : 2 * per_relay]).astype(jnp.int32)
    groups = send_lists.reshape(ent_count, per_relay)
    slots = bit_reverse(groups ^ lax.axis_index("grp"), grp_bits)
    shifts = (my_ent - jnp.arange(ent_count, dtype=jnp.int32)) % ent_count
    rows_in = arrived.shape[1]

    grid_spec = pltpu.PrefetchScalarGridSpec(
        num_scalar_prefetch=4,
        grid=(ent_count,),
        in_specs=[
            pl.BlockSpec((1, rows_in, block), lambda e, c, g, s, k: (e, 0, 0)),
            pl.BlockSpec(memory_space=pltpu.VMEM),
            pl.BlockSpec(memory_space=pltpu.VMEM),
        ],
        out_specs=[
            pl.BlockSpec((1, block, width), lambda e, c, g, s, k: (k[e], 0, 0)),
            pl.BlockSpec((grp_count // 2, block, width), lambda e, c, g, s, k: (0, 0, 0)),
            pl.BlockSpec((grp_count // 2, block, width), lambda e, c, g, s, k: (0, 0, 0)),
        ],
    )
    row_parts, owner_keep, owner_send = pl.pallas_call(
        lambda *refs: tile_kernel(*refs, per_relay=per_relay, block=block),
        grid_spec=grid_spec,
        out_shape=[
            jax.ShapeDtypeStruct((ent_count, block, width), jnp.float32),
            jax.ShapeDtypeStruct((grp_count // 2, block, width), jnp.float32),
            jax.ShapeDtypeStruct((grp_count // 2, block, width), jnp.float32),
        ],
    )(codes, groups, slots, shifts, arrived, cores, group_blocks)

    rows = row_parts[0]
    for k in range(1, ent_count):
        rows = rows + shift_ent(row_parts[k], -k, ent_count)
    owner_part = grp_reduce_scatter(owner_keep, owner_send, grp_count)
    return rows + owner_part


def solution(mesh):
    in_specs = (
        P(("grp", "ent"), None),
        P(),
        P(("grp", "ent"), None, None),
        P(("grp", "ent"), None),
        P(("grp", "ent")),
        P(("grp", "ent"), None, None),
    )
    out_specs = P(("grp", "ent"), None)
    return jax.shard_map(
        on_device, mesh=mesh, in_specs=in_specs, out_specs=out_specs, check_vma=False
    )
```

```python
import jax
import jax.numpy as jnp
from jax import lax
from jax.experimental import pallas as pl
from jax.experimental.pallas import tpu as pltpu
from jax.sharding import PartitionSpec as P

LOSS_SCALE = 0.0625


def bit_reverse(values, bits):
    out = jnp.zeros_like(values)
    for b in range(bits):
        out = out | (((values >> b) & 1) << (bits - 1 - b))
    return out


def grp_reduce_scatter(keep, send, grp_count):
    parts = keep + lax.ppermute(send, "grp", [(i, i ^ 1) for i in range(grp_count)])
    bit = 2
    while bit < grp_count:
        half = parts.shape[0] // 2
        got = lax.ppermute(parts[half:], "grp", [(i, i ^ bit) for i in range(grp_count)])
        parts = parts[:half] + got
        bit *= 2
    return parts[0]


def grp_gather(block, grp_count):
    me = lax.axis_index("grp")
    held = block[None]
    bit = 1
    while bit < grp_count:
        got = lax.ppermute(held, "grp", [(i, i ^ bit) for i in range(grp_count)])
        low = (me // bit) % 2 == 0
        held = jnp.where(
            low, jnp.concatenate([held, got], axis=0), jnp.concatenate([got, held], axis=0)
        )
        bit *= 2
    return held


def shift_ent(x, shift, ent_count):
    return lax.ppermute(x, "ent", [(i, (i + shift) % ent_count) for i in range(ent_count)])


def tile_kernel(srcs_ref, codes_ref, groups_ref, slots_ref, in_ref, core_ref, panel_ref,
                keep_in_ref, send_in_ref, row_ref, keep_ref, send_ref, *, per_relay, block):
    e = srcs_ref[pl.program_id(0)]

    @pl.when(pl.program_id(0) == 0)
    def _():
        keep_ref[...] = keep_in_ref[...]
        send_ref[...] = send_in_ref[...]

    nt = (((1,), (1,)), ((), ()))
    base = per_relay * block
    own = jnp.concatenate(
        [in_ref[0, base : base + block, :], in_ref[0, base + block : base + 2 * block, :]], axis=1
    )
    half = keep_ref.shape[0]
    codes = [codes_ref[e, j] for j in range(per_relay)]
    rels = [c // 2 for c in codes]
    groups = [groups_ref[e, j] for j in range(per_relay)]
    mapped = [
        jnp.dot(own, core_ref[r], preferred_element_type=jnp.float32).astype(jnp.bfloat16)
        for r in rels
    ]
    predicted = [
        lax.dot_general(m, panel_ref[g], nt, preferred_element_type=jnp.float32)
        for m, g in zip(mapped, groups)
    ]
    resids = []
    for j in range(per_relay):
        scale = LOSS_SCALE * (codes[j] % 2).astype(jnp.float32)
        adj = in_ref[0, j * block : (j + 1) * block, :].astype(jnp.float32)
        resids.append(((predicted[j] - adj) * scale).astype(jnp.bfloat16))
    products = [
        jnp.dot(r, panel_ref[g], preferred_element_type=jnp.float32).astype(jnp.bfloat16)
        for r, g in zip(resids, groups)
    ]
    columns = [
        jnp.dot(
            r.astype(jnp.float32).T.astype(jnp.bfloat16), m, preferred_element_type=jnp.float32
        ).astype(jnp.bfloat16)
        for r, m in zip(resids, mapped)
    ]
    acc = None
    for p, r in zip(products, rels):
        part = lax.dot_general(p, core_ref[r], nt, preferred_element_type=jnp.float32)
        acc = part if acc is None else acc + part
    for j, c in enumerate(columns):
        slot = slots_ref[e, j]
        column = c.astype(jnp.float32)

        @pl.when(slot < half)
        def _():
            keep_ref[jnp.minimum(slot, half - 1)] += column

        @pl.when(slot >= half)
        def _():
            send_ref[jnp.maximum(slot - half, 0)] += column

    row_ref[0] = acc


def on_device(factor, cores, adjacency, tile_rels, tile_count, send_lists):
    ent_count = lax.axis_size("ent")
    grp_count = lax.axis_size("grp")
    my_ent = lax.axis_index("ent")
    tiles = tile_rels.shape[1]
    block = factor.shape[0]
    width = factor.shape[1]
    per_relay = tiles // ent_count
    head_rows = 16
    count = ent_count * per_relay
    grp_bits = grp_count.bit_length() - 1
    relations = cores.shape[0]

    relay_ids = jnp.arange(ent_count, dtype=jnp.int32)
    slot_ids = jnp.arange(per_relay, dtype=jnp.int32)
    tile_of = slot_ids[None, :] * ent_count + (relay_ids[:, None] - my_ent) % ent_count
    adj_out = adjacency[tile_of].astype(jnp.bfloat16).reshape(ent_count, per_relay * block, block)
    halves = jnp.concatenate([factor[:, :block], factor[:, block:]], axis=0)
    head = jnp.concatenate(
        [tile_rels.reshape(tiles)[tile_of].astype(jnp.float32),
         (tile_of < tile_count.reshape(())).astype(jnp.float32)],
        axis=1,
    )
    head = jnp.pad(head, ((0, 0), (0, block - 2 * per_relay)))
    head = jnp.broadcast_to(head[:, None, :], (ent_count, head_rows, block)).astype(jnp.bfloat16)
    outgoing = jnp.concatenate(
        [adj_out, jnp.broadcast_to(halves[None], (ent_count,) + halves.shape), head], axis=1
    )
    arrived = lax.all_to_all(outgoing, "ent", split_axis=0, concat_axis=0, tiled=True)
    group_blocks = grp_gather(factor, grp_count)

    def codes_of(buf):
        heads = buf[:, -head_rows].astype(jnp.float32)
        return (heads[:, :per_relay] * 2 + heads[:, per_relay : 2 * per_relay]).astype(jnp.int32)

    groups = send_lists.reshape(ent_count, per_relay)
    slots = bit_reverse(groups ^ lax.axis_index("grp"), grp_bits)
    rows_in = outgoing.shape[1]
    half = grp_count // 2

    def relay_tiles(srcs, codes, buf, keep, send):
        steps = srcs.shape[0]
        any_map = lambda i, *refs: (0, 0, 0)
        return pl.pallas_call(
            lambda *refs: tile_kernel(*refs, per_relay=per_relay, block=block),
            grid_spec=pltpu.PrefetchScalarGridSpec(
                num_scalar_prefetch=4,
                grid=(steps,),
                in_specs=[
                    pl.BlockSpec((1, rows_in, block), lambda i, e, c, g, s: (e[i], 0, 0)),
                    pl.BlockSpec(memory_space=pltpu.VMEM),
                    pl.BlockSpec(memory_space=pltpu.VMEM),
                    pl.BlockSpec((half, block, width), any_map),
                    pl.BlockSpec((half, block, width), any_map),
                ],
                out_specs=[
                    pl.BlockSpec((1, block, width), lambda i, *refs: (i, 0, 0)),
                    pl.BlockSpec((half, block, width), any_map),
                    pl.BlockSpec((half, block, width), any_map),
                ],
            ),
            out_shape=[
                jax.ShapeDtypeStruct((steps, block, width), jnp.float32),
                jax.ShapeDtypeStruct((half, block, width), jnp.float32),
                jax.ShapeDtypeStruct((half, block, width), jnp.float32),
            ],
        )(srcs, codes, groups, slots, buf, cores, group_blocks, keep, send)

    empty = jnp.zeros((half, block, width), jnp.float32)
    own_row, keep, send = relay_tiles(
        my_ent.reshape(1).astype(jnp.int32), codes_of(outgoing), outgoing, empty, empty
    )
    remote_srcs = (my_ent - jnp.arange(1, ent_count, dtype=jnp.int32)) % ent_count
    row_parts, keep, send = relay_tiles(remote_srcs, codes_of(arrived), arrived, keep, send)

    rows = own_row[0]
    for k in range(1, ent_count):
        rows = rows + shift_ent(row_parts[k - 1], -k, ent_count)
    owner_part = grp_reduce_scatter(keep, send, grp_count)
    return rows + owner_part


def solution(mesh):
    in_specs = (
        P(("grp", "ent"), None),
        P(),
        P(("grp", "ent"), None, None),
        P(("grp", "ent"), None),
        P(("grp", "ent")),
        P(("grp", "ent"), None, None),
    )
    out_specs = P(("grp", "ent"), None)
    return jax.shard_map(
        on_device, mesh=mesh, in_specs=in_specs, out_specs=out_specs, check_vma=False
    )
```

```python
import jax
import jax.numpy as jnp
from jax import lax
from jax.experimental import pallas as pl
from jax.experimental.pallas import tpu as pltpu
from jax.sharding import PartitionSpec as P

LOSS_SCALE = 0.0625


def bit_reverse(values, bits):
    out = jnp.zeros_like(values)
    for b in range(bits):
        out = out | (((values >> b) & 1) << (bits - 1 - b))
    return out


def grp_reduce_scatter(keep, send, grp_count):
    parts = keep + lax.ppermute(send, "grp", [(i, i ^ 1) for i in range(grp_count)])
    bit = 2
    while bit < grp_count:
        half = parts.shape[0] // 2
        got = lax.ppermute(parts[half:], "grp", [(i, i ^ bit) for i in range(grp_count)])
        parts = parts[:half] + got
        bit *= 2
    return parts[0]


def grp_gather(block, grp_count):
    me = lax.axis_index("grp")
    held = block[None]
    bit = 1
    while bit < grp_count:
        got = lax.ppermute(held, "grp", [(i, i ^ bit) for i in range(grp_count)])
        low = (me // bit) % 2 == 0
        held = jnp.where(
            low, jnp.concatenate([held, got], axis=0), jnp.concatenate([got, held], axis=0)
        )
        bit *= 2
    return held


def shift_ent(x, shift, ent_count):
    return lax.ppermute(x, "ent", [(i, (i + shift) % ent_count) for i in range(ent_count)])


def tile_kernel(srcs_ref, codes_ref, groups_ref, slots_ref, in_ref, core_ref, panel_ref,
                keep_in_ref, send_in_ref, row_ref, keep_ref, send_ref, *, per_relay, block):
    e = srcs_ref[pl.program_id(0)]

    @pl.when(pl.program_id(0) == 0)
    def _():
        keep_ref[...] = keep_in_ref[...]
        send_ref[...] = send_in_ref[...]

    nt = (((1,), (1,)), ((), ()))
    base = per_relay * block
    own = jnp.concatenate(
        [in_ref[0, base : base + block, :], in_ref[0, base + block : base + 2 * block, :]], axis=1
    )
    half = keep_ref.shape[0]
    codes = [codes_ref[e, j] for j in range(per_relay)]
    rels = [c // 2 for c in codes]
    groups = [groups_ref[e, j] for j in range(per_relay)]
    mapped = [
        jnp.dot(own, core_ref[r], preferred_element_type=jnp.float32).astype(jnp.bfloat16)
        for r in rels
    ]
    predicted = [
        lax.dot_general(m, panel_ref[g], nt, preferred_element_type=jnp.float32)
        for m, g in zip(mapped, groups)
    ]
    resids = []
    for j in range(per_relay):
        scale = LOSS_SCALE * (codes[j] % 2).astype(jnp.float32)
        adj = in_ref[0, j * block : (j + 1) * block, :].astype(jnp.float32)
        resids.append(((predicted[j] - adj) * scale).astype(jnp.bfloat16))
    products = [
        jnp.dot(r, panel_ref[g], preferred_element_type=jnp.float32).astype(jnp.bfloat16)
        for r, g in zip(resids, groups)
    ]
    columns = [
        jnp.dot(
            r.astype(jnp.float32).T.astype(jnp.bfloat16), m, preferred_element_type=jnp.float32
        ).astype(jnp.bfloat16)
        for r, m in zip(resids, mapped)
    ]
    acc = None
    for p, r in zip(products, rels):
        part = lax.dot_general(p, core_ref[r], nt, preferred_element_type=jnp.float32)
        acc = part if acc is None else acc + part
    for j, c in enumerate(columns):
        slot = slots_ref[e, j]
        column = c.astype(jnp.float32)

        @pl.when(slot < half)
        def _():
            keep_ref[jnp.minimum(slot, half - 1)] += column

        @pl.when(slot >= half)
        def _():
            send_ref[jnp.maximum(slot - half, 0)] += column

    row_ref[0] = acc


def on_device(factor, cores, adjacency, tile_rels, tile_count, send_lists):
    ent_count = lax.axis_size("ent")
    grp_count = lax.axis_size("grp")
    my_ent = lax.axis_index("ent")
    tiles = tile_rels.shape[1]
    block = factor.shape[0]
    width = factor.shape[1]
    per_relay = tiles // ent_count
    head_rows = 16
    count = ent_count * per_relay
    grp_bits = grp_count.bit_length() - 1
    relations = cores.shape[0]

    relay_ids = jnp.arange(ent_count, dtype=jnp.int32)
    slot_ids = jnp.arange(per_relay, dtype=jnp.int32)
    tile_of = slot_ids[None, :] * ent_count + (relay_ids[:, None] - my_ent) % ent_count
    adj_out = adjacency[tile_of].astype(jnp.bfloat16).reshape(ent_count, per_relay * block, block)
    halves = jnp.concatenate([factor[:, :block], factor[:, block:]], axis=0)
    head = jnp.concatenate(
        [
            jnp.sum(
                jnp.where(
                    jnp.arange(tiles, dtype=jnp.int32) == tile_of[:, :, None],
                    tile_rels.reshape(1, 1, tiles),
                    0,
                ),
                axis=2,
            ).astype(jnp.float32),
         (tile_of < tile_count.reshape(())).astype(jnp.float32)],
        axis=1,
    )
    head = jnp.pad(head, ((0, 0), (0, block - 2 * per_relay)))
    head = jnp.broadcast_to(head[:, None, :], (ent_count, head_rows, block)).astype(jnp.bfloat16)
    outgoing = jnp.concatenate(
        [adj_out, jnp.broadcast_to(halves[None], (ent_count,) + halves.shape), head], axis=1
    )
    arrived = lax.all_to_all(outgoing, "ent", split_axis=0, concat_axis=0, tiled=True)
    group_blocks = grp_gather(factor, grp_count)

    def codes_of(buf):
        heads = buf[:, -head_rows].astype(jnp.float32)
        return (heads[:, :per_relay] * 2 + heads[:, per_relay : 2 * per_relay]).astype(jnp.int32)

    groups = send_lists.reshape(ent_count, per_relay)
    slots = bit_reverse(groups ^ lax.axis_index("grp"), grp_bits)
    rows_in = outgoing.shape[1]
    half = grp_count // 2

    def relay_tiles(srcs, codes, buf, keep, send):
        steps = srcs.shape[0]
        any_map = lambda i, *refs: (0, 0, 0)
        return pl.pallas_call(
            lambda *refs: tile_kernel(*refs, per_relay=per_relay, block=block),
            grid_spec=pltpu.PrefetchScalarGridSpec(
                num_scalar_prefetch=4,
                grid=(steps,),
                in_specs=[
                    pl.BlockSpec((1, rows_in, block), lambda i, e, c, g, s: (e[i], 0, 0)),
                    pl.BlockSpec(memory_space=pltpu.VMEM),
                    pl.BlockSpec(memory_space=pltpu.VMEM),
                    pl.BlockSpec((half, block, width), any_map),
                    pl.BlockSpec((half, block, width), any_map),
                ],
                out_specs=[
                    pl.BlockSpec((1, block, width), lambda i, *refs: (i, 0, 0)),
                    pl.BlockSpec((half, block, width), any_map),
                    pl.BlockSpec((half, block, width), any_map),
                ],
            ),
            out_shape=[
                jax.ShapeDtypeStruct((steps, block, width), jnp.float32),
                jax.ShapeDtypeStruct((half, block, width), jnp.float32),
                jax.ShapeDtypeStruct((half, block, width), jnp.float32),
            ],
        )(srcs, codes, groups, slots, buf, cores, group_blocks, keep, send)

    empty = jnp.zeros((half, block, width), jnp.float32)
    own_row, keep, send = relay_tiles(
        my_ent.reshape(1).astype(jnp.int32), codes_of(outgoing), outgoing, empty, empty
    )
    remote_srcs = (my_ent - jnp.arange(1, ent_count, dtype=jnp.int32)) % ent_count
    row_parts, keep, send = relay_tiles(remote_srcs, codes_of(arrived), arrived, keep, send)

    rows = own_row[0]
    for k in range(1, ent_count):
        rows = rows + shift_ent(row_parts[k - 1], -k, ent_count)
    owner_part = grp_reduce_scatter(keep, send, grp_count)
    return rows + owner_part


def solution(mesh):
    in_specs = (
        P(("grp", "ent"), None),
        P(),
        P(("grp", "ent"), None, None),
        P(("grp", "ent"), None),
        P(("grp", "ent")),
        P(("grp", "ent"), None, None),
    )
    out_specs = P(("grp", "ent"), None)
    return jax.shard_map(
        on_device, mesh=mesh, in_specs=in_specs, out_specs=out_specs, check_vma=False
    )
```

```python
import jax
import jax.numpy as jnp
from jax import lax
from jax.experimental import pallas as pl
from jax.experimental.pallas import tpu as pltpu
from jax.sharding import PartitionSpec as P

LOSS_SCALE = 0.0625


def bit_reverse(values, bits):
    out = jnp.zeros_like(values)
    for b in range(bits):
        out = out | (((values >> b) & 1) << (bits - 1 - b))
    return out


def grp_reduce_scatter(keep, send, grp_count):
    parts = keep + lax.ppermute(send, "grp", [(i, i ^ 1) for i in range(grp_count)])
    bit = 2
    while bit < grp_count:
        half = parts.shape[0] // 2
        got = lax.ppermute(parts[half:], "grp", [(i, i ^ bit) for i in range(grp_count)])
        parts = parts[:half] + got
        bit *= 2
    return parts[0]


def grp_gather(block, grp_count):
    me = lax.axis_index("grp")
    held = block[None]
    bit = 1
    while bit < grp_count:
        got = lax.ppermute(held, "grp", [(i, i ^ bit) for i in range(grp_count)])
        low = (me // bit) % 2 == 0
        held = jnp.where(
            low, jnp.concatenate([held, got], axis=0), jnp.concatenate([got, held], axis=0)
        )
        bit *= 2
    return held


def shift_ent(x, shift, ent_count):
    return lax.ppermute(x, "ent", [(i, (i + shift) % ent_count) for i in range(ent_count)])


def tile_kernel(srcs_ref, codes_ref, groups_ref, slots_ref, in_ref, core_ref, panel_ref,
                keep_in_ref, send_in_ref, row_ref, keep_ref, send_ref, *, per_relay, block):
    e = srcs_ref[pl.program_id(0)]

    @pl.when(pl.program_id(0) == 0)
    def _():
        keep_ref[...] = keep_in_ref[...]
        send_ref[...] = send_in_ref[...]

    nt = (((1,), (1,)), ((), ()))
    base = per_relay * block
    own = jnp.concatenate(
        [in_ref[0, base : base + block, :], in_ref[0, base + block : base + 2 * block, :]], axis=1
    )
    half = keep_ref.shape[0]
    codes = [codes_ref[pl.program_id(0), j] for j in range(per_relay)]
    rels = [c // 2 for c in codes]
    groups = [groups_ref[e, j] for j in range(per_relay)]
    mapped = [
        jnp.dot(own, core_ref[r], preferred_element_type=jnp.float32).astype(jnp.bfloat16)
        for r in rels
    ]
    predicted = [
        lax.dot_general(m, panel_ref[g], nt, preferred_element_type=jnp.float32)
        for m, g in zip(mapped, groups)
    ]
    resids = []
    for j in range(per_relay):
        scale = LOSS_SCALE * (codes[j] % 2).astype(jnp.float32)
        adj = in_ref[0, j * block : (j + 1) * block, :].astype(jnp.float32)
        resids.append(((predicted[j] - adj) * scale).astype(jnp.bfloat16))
    products = [
        jnp.dot(r, panel_ref[g], preferred_element_type=jnp.float32).astype(jnp.bfloat16)
        for r, g in zip(resids, groups)
    ]
    columns = [
        jnp.dot(
            r.astype(jnp.float32).T.astype(jnp.bfloat16), m, preferred_element_type=jnp.float32
        ).astype(jnp.bfloat16)
        for r, m in zip(resids, mapped)
    ]
    acc = None
    for p, r in zip(products, rels):
        part = lax.dot_general(p, core_ref[r], nt, preferred_element_type=jnp.float32)
        acc = part if acc is None else acc + part
    for j, c in enumerate(columns):
        slot = slots_ref[e, j]
        column = c.astype(jnp.float32)

        @pl.when(slot < half)
        def _():
            keep_ref[jnp.minimum(slot, half - 1)] += column

        @pl.when(slot >= half)
        def _():
            send_ref[jnp.maximum(slot - half, 0)] += column

    row_ref[0] = acc


def on_device(factor, cores, adjacency, tile_rels, tile_count, send_lists):
    ent_count = lax.axis_size("ent")
    grp_count = lax.axis_size("grp")
    my_ent = lax.axis_index("ent")
    tiles = tile_rels.shape[1]
    block = factor.shape[0]
    width = factor.shape[1]
    per_relay = tiles // ent_count
    count = ent_count * per_relay
    grp_bits = grp_count.bit_length() - 1
    relations = cores.shape[0]

    relay_ids = jnp.arange(ent_count, dtype=jnp.int32)
    slot_ids = jnp.arange(per_relay, dtype=jnp.int32)
    tile_of = slot_ids[None, :] * ent_count + (relay_ids[:, None] - my_ent) % ent_count
    adj_out = adjacency[tile_of].astype(jnp.bfloat16).reshape(ent_count, per_relay * block, block)
    halves = jnp.concatenate([factor[:, :block], factor[:, block:]], axis=0)
    outgoing = jnp.concatenate(
        [adj_out, jnp.broadcast_to(halves[None], (ent_count,) + halves.shape)], axis=1
    )
    arrived = lax.all_to_all(outgoing, "ent", split_axis=0, concat_axis=0, tiled=True)
    group_blocks = grp_gather(factor, grp_count)
    picked = jnp.sum(
        jnp.where(
            jnp.arange(tiles, dtype=jnp.int32) == tile_of[:, :, None],
            tile_rels.reshape(1, 1, tiles),
            0,
        ),
        axis=2,
    )
    codes_out = picked * 2 + (tile_of < tile_count.reshape(())).astype(jnp.int32)
    codes_in = jnp.stack(
        [
            shift_ent(codes_out[(my_ent + k) % ent_count], k, ent_count)
            for k in range(1, ent_count)
        ]
    )

    groups = send_lists.reshape(ent_count, per_relay)
    slots = bit_reverse(groups ^ lax.axis_index("grp"), grp_bits)
    rows_in = outgoing.shape[1]
    half = grp_count // 2

    def relay_tiles(srcs, codes, buf, keep, send):
        steps = srcs.shape[0]
        any_map = lambda i, *refs: (0, 0, 0)
        return pl.pallas_call(
            lambda *refs: tile_kernel(*refs, per_relay=per_relay, block=block),
            grid_spec=pltpu.PrefetchScalarGridSpec(
                num_scalar_prefetch=4,
                grid=(steps,),
                in_specs=[
                    pl.BlockSpec((1, rows_in, block), lambda i, e, c, g, s: (e[i], 0, 0)),
                    pl.BlockSpec(memory_space=pltpu.VMEM),
                    pl.BlockSpec(memory_space=pltpu.VMEM),
                    pl.BlockSpec((half, block, width), any_map),
                    pl.BlockSpec((half, block, width), any_map),
                ],
                out_specs=[
                    pl.BlockSpec((1, block, width), lambda i, *refs: (i, 0, 0)),
                    pl.BlockSpec((half, block, width), any_map),
                    pl.BlockSpec((half, block, width), any_map),
                ],
            ),
            out_shape=[
                jax.ShapeDtypeStruct((steps, block, width), jnp.float32),
                jax.ShapeDtypeStruct((half, block, width), jnp.float32),
                jax.ShapeDtypeStruct((half, block, width), jnp.float32),
            ],
        )(srcs, codes, groups, slots, buf, cores, group_blocks, keep, send)

    empty = jnp.zeros((half, block, width), jnp.float32)
    own_row, keep, send = relay_tiles(
        my_ent.reshape(1).astype(jnp.int32), codes_out[my_ent][None], outgoing, empty, empty
    )
    remote_srcs = (my_ent - jnp.arange(1, ent_count, dtype=jnp.int32)) % ent_count
    row_parts, keep, send = relay_tiles(remote_srcs, codes_in, arrived, keep, send)

    rows = own_row[0]
    for k in range(1, ent_count):
        rows = rows + shift_ent(row_parts[k - 1], -k, ent_count)
    owner_part = grp_reduce_scatter(keep, send, grp_count)
    return rows + owner_part


def solution(mesh):
    in_specs = (
        P(("grp", "ent"), None),
        P(),
        P(("grp", "ent"), None, None),
        P(("grp", "ent"), None),
        P(("grp", "ent")),
        P(("grp", "ent"), None, None),
    )
    out_specs = P(("grp", "ent"), None)
    return jax.shard_map(
        on_device, mesh=mesh, in_specs=in_specs, out_specs=out_specs, check_vma=False
    )
```

```python
import jax
import jax.numpy as jnp
from jax import lax
from jax.experimental import pallas as pl
from jax.experimental.pallas import tpu as pltpu
from jax.sharding import PartitionSpec as P

LOSS_SCALE = 0.0625


def bit_reverse(values, bits):
    out = jnp.zeros_like(values)
    for b in range(bits):
        out = out | (((values >> b) & 1) << (bits - 1 - b))
    return out


def grp_reduce_scatter(keep, send, grp_count):
    got = lax.ppermute(send, "grp", [(i, i ^ 1) for i in range(grp_count)])
    bit = 2
    while bit < grp_count:
        half = keep.shape[0] // 2
        outgoing = keep[half:] + got[half:]
        keep = keep[:half] + got[:half]
        got = lax.ppermute(outgoing, "grp", [(i, i ^ bit) for i in range(grp_count)])
        bit *= 2
    return (keep + got)[0]


def grp_gather(block, grp_count):
    me = lax.axis_index("grp")
    held = block[None]
    bit = 1
    while bit < grp_count:
        got = lax.ppermute(held, "grp", [(i, i ^ bit) for i in range(grp_count)])
        low = (me // bit) % 2 == 0
        held = jnp.where(
            low, jnp.concatenate([held, got], axis=0), jnp.concatenate([got, held], axis=0)
        )
        bit *= 2
    return held


def shift_ent(x, shift, ent_count):
    return lax.ppermute(x, "ent", [(i, (i + shift) % ent_count) for i in range(ent_count)])


def tile_kernel(srcs_ref, codes_ref, groups_ref, slots_ref, in_ref, core_ref, panel_ref,
                keep_in_ref, send_in_ref, row_ref, keep_ref, send_ref, *, per_relay, block):
    e = srcs_ref[pl.program_id(0)]

    @pl.when(pl.program_id(0) == 0)
    def _():
        keep_ref[...] = keep_in_ref[...]
        send_ref[...] = send_in_ref[...]

    nt = (((1,), (1,)), ((), ()))
    base = per_relay * block
    own = jnp.concatenate(
        [in_ref[0, base : base + block, :], in_ref[0, base + block : base + 2 * block, :]], axis=1
    )
    half = keep_ref.shape[0]
    codes = [codes_ref[e, j] for j in range(per_relay)]
    rels = [c // 2 for c in codes]
    groups = [groups_ref[e, j] for j in range(per_relay)]
    mapped = [
        jnp.dot(own, core_ref[r], preferred_element_type=jnp.float32).astype(jnp.bfloat16)
        for r in rels
    ]
    predicted = [
        lax.dot_general(m, panel_ref[g], nt, preferred_element_type=jnp.float32)
        for m, g in zip(mapped, groups)
    ]
    resids = []
    for j in range(per_relay):
        scale = LOSS_SCALE * (codes[j] % 2).astype(jnp.float32)
        adj = in_ref[0, j * block : (j + 1) * block, :].astype(jnp.float32)
        resids.append(((predicted[j] - adj) * scale).astype(jnp.bfloat16))
    products = [
        jnp.dot(r, panel_ref[g], preferred_element_type=jnp.float32).astype(jnp.bfloat16)
        for r, g in zip(resids, groups)
    ]
    columns = [
        jnp.dot(
            r.astype(jnp.float32).T.astype(jnp.bfloat16), m, preferred_element_type=jnp.float32
        ).astype(jnp.bfloat16)
        for r, m in zip(resids, mapped)
    ]
    acc = None
    for p, r in zip(products, rels):
        part = lax.dot_general(p, core_ref[r], nt, preferred_element_type=jnp.float32)
        acc = part if acc is None else acc + part
    for j, c in enumerate(columns):
        slot = slots_ref[e, j]
        column = c.astype(jnp.float32)

        @pl.when(slot < half)
        def _():
            keep_ref[jnp.minimum(slot, half - 1)] += column

        @pl.when(slot >= half)
        def _():
            send_ref[jnp.maximum(slot - half, 0)] += column

    row_ref[0] = acc


def on_device(factor, cores, adjacency, tile_rels, tile_count, send_lists):
    ent_count = lax.axis_size("ent")
    grp_count = lax.axis_size("grp")
    my_ent = lax.axis_index("ent")
    tiles = tile_rels.shape[1]
    block = factor.shape[0]
    width = factor.shape[1]
    per_relay = tiles // ent_count
    head_rows = 16
    count = ent_count * per_relay
    grp_bits = grp_count.bit_length() - 1
    relations = cores.shape[0]

    relay_ids = jnp.arange(ent_count, dtype=jnp.int32)
    slot_ids = jnp.arange(per_relay, dtype=jnp.int32)
    tile_of = slot_ids[None, :] * ent_count + (relay_ids[:, None] - my_ent) % ent_count
    adj_out = adjacency[tile_of].astype(jnp.bfloat16).reshape(ent_count, per_relay * block, block)
    halves = jnp.concatenate([factor[:, :block], factor[:, block:]], axis=0)
    head = jnp.concatenate(
        [
            jnp.sum(
                jnp.where(
                    jnp.arange(tiles, dtype=jnp.int32) == tile_of[:, :, None],
                    tile_rels.reshape(1, 1, tiles),
                    0,
                ),
                axis=2,
            ).astype(jnp.float32),
         (tile_of < tile_count.reshape(())).astype(jnp.float32)],
        axis=1,
    )
    head = jnp.pad(head, ((0, 0), (0, block - 2 * per_relay)))
    head = jnp.broadcast_to(head[:, None, :], (ent_count, head_rows, block)).astype(jnp.bfloat16)
    outgoing = jnp.concatenate(
        [adj_out, jnp.broadcast_to(halves[None], (ent_count,) + halves.shape), head], axis=1
    )
    arrived = lax.all_to_all(outgoing, "ent", split_axis=0, concat_axis=0, tiled=True)
    group_blocks = grp_gather(factor, grp_count)

    def codes_of(buf):
        heads = buf[:, -head_rows].astype(jnp.float32)
        return (heads[:, :per_relay] * 2 + heads[:, per_relay : 2 * per_relay]).astype(jnp.int32)

    groups = send_lists.reshape(ent_count, per_relay)
    slots = bit_reverse(groups ^ lax.axis_index("grp"), grp_bits)
    rows_in = outgoing.shape[1]
    half = grp_count // 2

    def relay_tiles(srcs, codes, buf, keep, send):
        steps = srcs.shape[0]
        any_map = lambda i, *refs: (0, 0, 0)
        return pl.pallas_call(
            lambda *refs: tile_kernel(*refs, per_relay=per_relay, block=block),
            grid_spec=pltpu.PrefetchScalarGridSpec(
                num_scalar_prefetch=4,
                grid=(steps,),
                in_specs=[
                    pl.BlockSpec((1, rows_in, block), lambda i, e, c, g, s: (e[i], 0, 0)),
                    pl.BlockSpec(memory_space=pltpu.VMEM),
                    pl.BlockSpec(memory_space=pltpu.VMEM),
                    pl.BlockSpec((half, block, width), any_map),
                    pl.BlockSpec((half, block, width), any_map),
                ],
                out_specs=[
                    pl.BlockSpec((1, block, width), lambda i, *refs: (i, 0, 0)),
                    pl.BlockSpec((half, block, width), any_map),
                    pl.BlockSpec((half, block, width), any_map),
                ],
            ),
            out_shape=[
                jax.ShapeDtypeStruct((steps, block, width), jnp.float32),
                jax.ShapeDtypeStruct((half, block, width), jnp.float32),
                jax.ShapeDtypeStruct((half, block, width), jnp.float32),
            ],
        )(srcs, codes, groups, slots, buf, cores, group_blocks, keep, send)

    empty = jnp.zeros((half, block, width), jnp.float32)
    own_row, keep, send = relay_tiles(
        my_ent.reshape(1).astype(jnp.int32), codes_of(outgoing), outgoing, empty, empty
    )
    remote_srcs = (my_ent - jnp.arange(1, ent_count, dtype=jnp.int32)) % ent_count
    row_parts, keep, send = relay_tiles(remote_srcs, codes_of(arrived), arrived, keep, send)

    rows = own_row[0]
    for k in range(1, ent_count):
        rows = rows + shift_ent(row_parts[k - 1], -k, ent_count)
    owner_part = grp_reduce_scatter(keep, send, grp_count)
    return rows + owner_part


def solution(mesh):
    in_specs = (
        P(("grp", "ent"), None),
        P(),
        P(("grp", "ent"), None, None),
        P(("grp", "ent"), None),
        P(("grp", "ent")),
        P(("grp", "ent"), None, None),
    )
    out_specs = P(("grp", "ent"), None)
    return jax.shard_map(
        on_device, mesh=mesh, in_specs=in_specs, out_specs=out_specs, check_vma=False
    )
```

```python
import jax
import jax.numpy as jnp
from jax import lax
from jax.experimental import pallas as pl
from jax.experimental.pallas import tpu as pltpu
from jax.sharding import PartitionSpec as P

LOSS_SCALE = 0.0625


def bit_reverse(values, bits):
    out = jnp.zeros_like(values)
    for b in range(bits):
        out = out | (((values >> b) & 1) << (bits - 1 - b))
    return out


def grp_reduce_scatter(keep, send, grp_count):
    parts = keep + lax.ppermute(send, "grp", [(i, i ^ 1) for i in range(grp_count)])
    bit = 2
    while bit < grp_count:
        half = parts.shape[0] // 2
        got = lax.ppermute(parts[half:], "grp", [(i, i ^ bit) for i in range(grp_count)])
        parts = parts[:half] + got
        bit *= 2
    return parts[0]


def grp_gather(block, grp_count):
    me = lax.axis_index("grp")
    held = block[None]
    bit = 1
    while bit < grp_count:
        got = lax.ppermute(held, "grp", [(i, i ^ bit) for i in range(grp_count)])
        low = (me // bit) % 2 == 0
        held = jnp.where(
            low, jnp.concatenate([held, got], axis=0), jnp.concatenate([got, held], axis=0)
        )
        bit *= 2
    return held


def shift_ent(x, shift, ent_count):
    return lax.ppermute(x, "ent", [(i, (i + shift) % ent_count) for i in range(ent_count)])


def tile_kernel(srcs_ref, codes_ref, groups_ref, slots_ref, in_ref, core_ref, panel_ref,
                keep_in_ref, send_in_ref, row_ref, keep_ref, send_ref, *, per_relay, block, steps):
    keep_ref[...] = keep_in_ref[...]
    send_ref[...] = send_in_ref[...]
    nt = (((1,), (1,)), ((), ()))
    base = per_relay * block
    half = keep_ref.shape[0]
    for i in range(steps):
        e = srcs_ref[i]
        own = jnp.concatenate(
            [in_ref[e, base : base + block, :], in_ref[e, base + block : base + 2 * block, :]],
            axis=1,
        )
        codes = [codes_ref[e, j] for j in range(per_relay)]
        rels = [c // 2 for c in codes]
        groups = [groups_ref[e, j] for j in range(per_relay)]
        mapped = [
            jnp.dot(own, core_ref[r], preferred_element_type=jnp.float32).astype(jnp.bfloat16)
            for r in rels
        ]
        predicted = [
            lax.dot_general(m, panel_ref[g], nt, preferred_element_type=jnp.float32)
            for m, g in zip(mapped, groups)
        ]
        resids = []
        for j in range(per_relay):
            scale = LOSS_SCALE * (codes[j] % 2).astype(jnp.float32)
            adj = in_ref[e, j * block : (j + 1) * block, :].astype(jnp.float32)
            resids.append(((predicted[j] - adj) * scale).astype(jnp.bfloat16))
        products = [
            jnp.dot(r, panel_ref[g], preferred_element_type=jnp.float32).astype(jnp.bfloat16)
            for r, g in zip(resids, groups)
        ]
        columns = [
            jnp.dot(
                r.astype(jnp.float32).T.astype(jnp.bfloat16), m,
                preferred_element_type=jnp.float32,
            ).astype(jnp.bfloat16)
            for r, m in zip(resids, mapped)
        ]
        acc = None
        for p, r in zip(products, rels):
            part = lax.dot_general(p, core_ref[r], nt, preferred_element_type=jnp.float32)
            acc = part if acc is None else acc + part
        for j, c in enumerate(columns):
            slot = slots_ref[e, j]
            column = c.astype(jnp.float32)

            @pl.when(slot < half)
            def _():
                keep_ref[jnp.minimum(slot, half - 1)] += column

            @pl.when(slot >= half)
            def _():
                send_ref[jnp.maximum(slot - half, 0)] += column

        row_ref[i] = acc


def on_device(factor, cores, adjacency, tile_rels, tile_count, send_lists):
    ent_count = lax.axis_size("ent")
    grp_count = lax.axis_size("grp")
    my_ent = lax.axis_index("ent")
    tiles = tile_rels.shape[1]
    block = factor.shape[0]
    width = factor.shape[1]
    per_relay = tiles // ent_count
    head_rows = 16
    count = ent_count * per_relay
    grp_bits = grp_count.bit_length() - 1
    relations = cores.shape[0]

    relay_ids = jnp.arange(ent_count, dtype=jnp.int32)
    slot_ids = jnp.arange(per_relay, dtype=jnp.int32)
    tile_of = slot_ids[None, :] * ent_count + (relay_ids[:, None] - my_ent) % ent_count
    adj_out = adjacency[tile_of].astype(jnp.bfloat16).reshape(ent_count, per_relay * block, block)
    halves = jnp.concatenate([factor[:, :block], factor[:, block:]], axis=0)
    head = jnp.concatenate(
        [
            jnp.sum(
                jnp.where(
                    jnp.arange(tiles, dtype=jnp.int32) == tile_of[:, :, None],
                    tile_rels.reshape(1, 1, tiles),
                    0,
                ),
                axis=2,
            ).astype(jnp.float32),
         (tile_of < tile_count.reshape(())).astype(jnp.float32)],
        axis=1,
    )
    head = jnp.pad(head, ((0, 0), (0, block - 2 * per_relay)))
    head = jnp.broadcast_to(head[:, None, :], (ent_count, head_rows, block)).astype(jnp.bfloat16)
    outgoing = jnp.concatenate(
        [adj_out, jnp.broadcast_to(halves[None], (ent_count,) + halves.shape), head], axis=1
    )
    arrived = lax.all_to_all(outgoing, "ent", split_axis=0, concat_axis=0, tiled=True)
    group_blocks = grp_gather(factor, grp_count)

    def codes_of(buf):
        heads = buf[:, -head_rows].astype(jnp.float32)
        return (heads[:, :per_relay] * 2 + heads[:, per_relay : 2 * per_relay]).astype(jnp.int32)

    groups = send_lists.reshape(ent_count, per_relay)
    slots = bit_reverse(groups ^ lax.axis_index("grp"), grp_bits)
    rows_in = outgoing.shape[1]
    half = grp_count // 2

    def relay_tiles(srcs, codes, buf, keep, send):
        steps = srcs.shape[0]
        any_map = lambda i, *refs: (0, 0, 0)
        return pl.pallas_call(
            lambda *refs: tile_kernel(*refs, per_relay=per_relay, block=block, steps=steps),
            grid_spec=pltpu.PrefetchScalarGridSpec(
                num_scalar_prefetch=4,
                grid=(1,),
                in_specs=[
                    pl.BlockSpec((ent_count, rows_in, block), any_map),
                    pl.BlockSpec(memory_space=pltpu.VMEM),
                    pl.BlockSpec(memory_space=pltpu.VMEM),
                    pl.BlockSpec((half, block, width), any_map),
                    pl.BlockSpec((half, block, width), any_map),
                ],
                out_specs=[
                    pl.BlockSpec((steps, block, width), any_map),
                    pl.BlockSpec((half, block, width), any_map),
                    pl.BlockSpec((half, block, width), any_map),
                ],
            ),
            out_shape=[
                jax.ShapeDtypeStruct((steps, block, width), jnp.float32),
                jax.ShapeDtypeStruct((half, block, width), jnp.float32),
                jax.ShapeDtypeStruct((half, block, width), jnp.float32),
            ],
        )(srcs, codes, groups, slots, buf, cores, group_blocks, keep, send)

    empty = jnp.zeros((half, block, width), jnp.float32)
    own_row, keep, send = relay_tiles(
        my_ent.reshape(1).astype(jnp.int32), codes_of(outgoing), outgoing, empty, empty
    )
    remote_srcs = (my_ent - jnp.arange(1, ent_count, dtype=jnp.int32)) % ent_count
    row_parts, keep, send = relay_tiles(remote_srcs, codes_of(arrived), arrived, keep, send)

    rows = own_row[0]
    for k in range(1, ent_count):
        rows = rows + shift_ent(row_parts[k - 1], -k, ent_count)
    owner_part = grp_reduce_scatter(keep, send, grp_count)
    return rows + owner_part


def solution(mesh):
    in_specs = (
        P(("grp", "ent"), None),
        P(),
        P(("grp", "ent"), None, None),
        P(("grp", "ent"), None),
        P(("grp", "ent")),
        P(("grp", "ent"), None, None),
    )
    out_specs = P(("grp", "ent"), None)
    return jax.shard_map(
        on_device, mesh=mesh, in_specs=in_specs, out_specs=out_specs, check_vma=False
    )
```

```python
import jax
import jax.numpy as jnp
from jax import lax
from jax.experimental import pallas as pl
from jax.experimental.pallas import tpu as pltpu
from jax.sharding import PartitionSpec as P

LOSS_SCALE = 0.0625


def bit_reverse(values, bits):
    out = jnp.zeros_like(values)
    for b in range(bits):
        out = out | (((values >> b) & 1) << (bits - 1 - b))
    return out


def grp_reduce_scatter(keep, send, grp_count):
    parts = keep + lax.ppermute(send, "grp", [(i, i ^ 1) for i in range(grp_count)])
    bit = 2
    while bit < grp_count:
        half = parts.shape[0] // 2
        got = lax.ppermute(parts[half:], "grp", [(i, i ^ bit) for i in range(grp_count)])
        parts = parts[:half] + got
        bit *= 2
    return parts[0]


def grp_gather(block, grp_count):
    me = lax.axis_index("grp")
    held = block[None]
    bit = 1
    while bit < grp_count:
        got = lax.ppermute(held, "grp", [(i, i ^ bit) for i in range(grp_count)])
        low = (me // bit) % 2 == 0
        held = jnp.where(
            low, jnp.concatenate([held, got], axis=0), jnp.concatenate([got, held], axis=0)
        )
        bit *= 2
    return held


def shift_ent(x, shift, ent_count):
    return lax.ppermute(x, "ent", [(i, (i + shift) % ent_count) for i in range(ent_count)])


def tile_kernel(srcs_ref, codes_ref, groups_ref, slots_ref, in_ref, core_ref, panel_ref,
                keep_in_ref, send_in_ref, row_ref, keep_ref, send_ref, *, per_relay, block):
    e = srcs_ref[pl.program_id(0)]

    @pl.when(pl.program_id(0) == 0)
    def _():
        keep_ref[...] = keep_in_ref[...]
        send_ref[...] = send_in_ref[...]

    nt = (((1,), (1,)), ((), ()))
    base = per_relay * block
    own = jnp.concatenate(
        [in_ref[0, base : base + block, :], in_ref[0, base + block : base + 2 * block, :]], axis=1
    )
    half = keep_ref.shape[0]
    codes = [codes_ref[e, j] for j in range(per_relay)]
    rels = [c // 2 for c in codes]
    groups = [groups_ref[e, j] for j in range(per_relay)]
    mapped = [
        jnp.dot(own, core_ref[r], preferred_element_type=jnp.float32).astype(jnp.bfloat16)
        for r in rels
    ]
    predicted = [
        lax.dot_general(m, panel_ref[g], nt, preferred_element_type=jnp.float32)
        for m, g in zip(mapped, groups)
    ]
    resids = []
    for j in range(per_relay):
        scale = LOSS_SCALE * (codes[j] % 2).astype(jnp.float32)
        adj = in_ref[0, j * block : (j + 1) * block, :].astype(jnp.float32)
        resids.append(((predicted[j] - adj) * scale).astype(jnp.bfloat16))
    products = [
        jnp.dot(r, panel_ref[g], preferred_element_type=jnp.float32).astype(jnp.bfloat16)
        for r, g in zip(resids, groups)
    ]
    columns = [
        jnp.dot(
            r.astype(jnp.float32).T.astype(jnp.bfloat16), m, preferred_element_type=jnp.float32
        ).astype(jnp.bfloat16)
        for r, m in zip(resids, mapped)
    ]
    acc = None
    for p, r in zip(products, rels):
        part = lax.dot_general(p, core_ref[r], nt, preferred_element_type=jnp.float32)
        acc = part if acc is None else acc + part
    for j, c in enumerate(columns):
        slot = slots_ref[e, j]
        column = c.astype(jnp.float32)

        @pl.when(slot < half)
        def _():
            keep_ref[jnp.minimum(slot, half - 1)] += column

        @pl.when(slot >= half)
        def _():
            send_ref[jnp.maximum(slot - half, 0)] += column

    row_ref[0] = acc


def build_kernel(tile_ref, rels_ref, count_ref, adj_ref, factor_ref, out_ref, *, per_relay,
                 block):
    u = pl.program_id(0)
    base = per_relay * block
    lane = lax.broadcasted_iota(jnp.int32, (16, block), 1)
    head = jnp.zeros((16, block), jnp.float32)
    for j in range(per_relay):
        t = tile_ref[u * per_relay + j]
        out_ref[0, j * block : (j + 1) * block, :] = adj_ref[t].astype(jnp.bfloat16)
        head = jnp.where(lane == j, rels_ref[t].astype(jnp.float32), head)
        live = (t < count_ref[0]).astype(jnp.float32)
        head = jnp.where(lane == per_relay + j, live, head)
    out_ref[0, base : base + block, :] = factor_ref[:, :block]
    out_ref[0, base + block : base + 2 * block, :] = factor_ref[:, block:]
    out_ref[0, base + 2 * block :, :] = head.astype(jnp.bfloat16)


def on_device(factor, cores, adjacency, tile_rels, tile_count, send_lists):
    ent_count = lax.axis_size("ent")
    grp_count = lax.axis_size("grp")
    my_ent = lax.axis_index("ent")
    tiles = tile_rels.shape[1]
    block = factor.shape[0]
    width = factor.shape[1]
    per_relay = tiles // ent_count
    head_rows = 16
    count = ent_count * per_relay
    grp_bits = grp_count.bit_length() - 1
    relations = cores.shape[0]

    relay_ids = jnp.arange(ent_count, dtype=jnp.int32)
    slot_ids = jnp.arange(per_relay, dtype=jnp.int32)
    tile_of = slot_ids[None, :] * ent_count + (relay_ids[:, None] - my_ent) % ent_count
    rows_out = per_relay * block + 2 * block + head_rows
    outgoing = pl.pallas_call(
        lambda *refs: build_kernel(*refs, per_relay=per_relay, block=block),
        grid_spec=pltpu.PrefetchScalarGridSpec(
            num_scalar_prefetch=3,
            grid=(ent_count,),
            in_specs=[
                pl.BlockSpec((tiles, block, block), lambda u, *refs: (0, 0, 0)),
                pl.BlockSpec((block, width), lambda u, *refs: (0, 0)),
            ],
            out_specs=pl.BlockSpec((1, rows_out, block), lambda u, *refs: (u, 0, 0)),
        ),
        out_shape=jax.ShapeDtypeStruct((ent_count, rows_out, block), jnp.bfloat16),
    )(tile_of.reshape(count), tile_rels.reshape(tiles), tile_count.reshape(1), adjacency, factor)
    arrived = lax.all_to_all(outgoing, "ent", split_axis=0, concat_axis=0, tiled=True)
    group_blocks = grp_gather(factor, grp_count)

    def codes_of(buf):
        heads = buf[:, -head_rows].astype(jnp.float32)
        return (heads[:, :per_relay] * 2 + heads[:, per_relay : 2 * per_relay]).astype(jnp.int32)

    groups = send_lists.reshape(ent_count, per_relay)
    slots = bit_reverse(groups ^ lax.axis_index("grp"), grp_bits)
    rows_in = outgoing.shape[1]
    half = grp_count // 2

    def relay_tiles(srcs, codes, buf, keep, send):
        steps = srcs.shape[0]
        any_map = lambda i, *refs: (0, 0, 0)
        return pl.pallas_call(
            lambda *refs: tile_kernel(*refs, per_relay=per_relay, block=block),
            grid_spec=pltpu.PrefetchScalarGridSpec(
                num_scalar_prefetch=4,
                grid=(steps,),
                in_specs=[
                    pl.BlockSpec((1, rows_in, block), lambda i, e, c, g, s: (e[i], 0, 0)),
                    pl.BlockSpec(memory_space=pltpu.VMEM),
                    pl.BlockSpec(memory_space=pltpu.VMEM),
                    pl.BlockSpec((half, block, width), any_map),
                    pl.BlockSpec((half, block, width), any_map),
                ],
                out_specs=[
                    pl.BlockSpec((1, block, width), lambda i, *refs: (i, 0, 0)),
                    pl.BlockSpec((half, block, width), any_map),
                    pl.BlockSpec((half, block, width), any_map),
                ],
            ),
            out_shape=[
                jax.ShapeDtypeStruct((steps, block, width), jnp.float32),
                jax.ShapeDtypeStruct((half, block, width), jnp.float32),
                jax.ShapeDtypeStruct((half, block, width), jnp.float32),
            ],
        )(srcs, codes, groups, slots, buf, cores, group_blocks, keep, send)

    empty = jnp.zeros((half, block, width), jnp.float32)
    own_row, keep, send = relay_tiles(
        my_ent.reshape(1).astype(jnp.int32), codes_of(outgoing), outgoing, empty, empty
    )
    remote_srcs = (my_ent - jnp.arange(1, ent_count, dtype=jnp.int32)) % ent_count
    row_parts, keep, send = relay_tiles(remote_srcs, codes_of(arrived), arrived, keep, send)

    rows = own_row[0]
    for k in range(1, ent_count):
        rows = rows + shift_ent(row_parts[k - 1], -k, ent_count)
    owner_part = grp_reduce_scatter(keep, send, grp_count)
    return rows + owner_part


def solution(mesh):
    in_specs = (
        P(("grp", "ent"), None),
        P(),
        P(("grp", "ent"), None, None),
        P(("grp", "ent"), None),
        P(("grp", "ent")),
        P(("grp", "ent"), None, None),
    )
    out_specs = P(("grp", "ent"), None)
    return jax.shard_map(
        on_device, mesh=mesh, in_specs=in_specs, out_specs=out_specs, check_vma=False
    )
```
